512 devices in a mesh: band: 16 (over y, x), pix: 32 (over z, core).
Axes of the slice: x: 4, y: 4, z: 16, core: 2. Of those that a mesh axis runs over, the one named last changes fastest.
Arguments:
- pixels: bfloat16 [512, 32, 1024], P('pix', 'band'), may hold values from -6 to 6
- clear_count: int32 [32], P('pix'), may hold values from 3 to 10, as said below
- clear_index: int32 [320], P('pix'), may hold values from 0 to 15, as said below
- attn_gain: float32 [1024], replicated, may hold values from 0.1 to 1.9
- w_query: bfloat16 [1024, 1024], P(None, 'band')
- w_key: bfloat16 [1024, 1024], P(None, 'band')
- w_value: bfloat16 [1024, 1024], P(None, 'band'), may hold values from -0.1875 to 0.1875
- w_out: bfloat16 [1024, 1024], P('band'), may hold values from -0.1875 to 0.1875
- mlp_gain: float32 [1024], replicated, may hold values from 0.1 to 1.9
- w_gate: bfloat16 [1024, 4096], P(None, 'band'), may hold values from -0.1875 to 0.1875
- w_up: bfloat16 [1024, 4096], P(None, 'band'), may hold values from -0.1875 to 0.1875
- w_down: bfloat16 [4096, 1024], P('band'), may hold values from -0.09375 to 0.09375
Outputs:
- updated: bfloat16 [512, 32, 1024], P('pix', 'band')
The draws below stay inside these ranges and needn't reach their ends.
Inputs may be any that keep to these rules, and one draw needn't show every extreme that they name: `clear_count`: some tile, drawn from the seed, keeps exactly 10 clear pixels. `clear_index`: for tile t, entries t*10 to t*10+clear_count[t]-1 are distinct local pixel indices in rising order; the tile's remaining entries are 0.
All inputs are finite; a program needn't handle non-finite values.
Results may differ from the reference program's by a relative error of at most 0.019.
Values may be sent and summed in bfloat16 or wider, within the bound.
No kernel may reach another device: no remote copies, remote signals or barrier semaphores. Data moves between devices by JAX's collectives and lax.ppermute only.
A program may use at most 64 MiB of HBM per device.

```python
import jax
import jax.numpy as jnp
from jax import lax

D = 1024
HEADS = 16
HD = 64
FF = 4096
PIX_DEV = 16
CAP = 10
MIN_KEEP = 3
SPEC = 32
PIXELS = 512
N_BAND = 16
N_PIX = 32


def coupled_pair(key):
    base = jax.random.normal(jax.random.fold_in(key, 11), (D, HEADS * HD), jnp.float32) * D ** (-0.5)
    other = jax.random.normal(jax.random.fold_in(key, 12), (D, HEADS * HD), jnp.float32) * D ** (-0.5)
    return (1.7 * base, 1.7 * other)


def draw_w_query(key, part):
    return coupled_pair(key)[0].astype(jnp.bfloat16)


def draw_w_key(key, part):
    return coupled_pair(key)[1].astype(jnp.bfloat16)


def clear_lists(key):
    counts = jax.random.randint(jax.random.fold_in(key, 21), (N_PIX,), MIN_KEEP, CAP + 1)
    full_tile = jax.random.randint(jax.random.fold_in(key, 22), (), 0, N_PIX)
    counts = jnp.where(jnp.arange(N_PIX) == full_tile, CAP, counts)
    scores = jax.random.randint(jax.random.fold_in(key, 23), (N_PIX, PIX_DEV), 0, 1 << 20)
    scores = scores * PIX_DEV + jnp.arange(PIX_DEV)[None, :]
    ranks = jnp.argsort(jnp.argsort(scores, axis=1), axis=1)
    chosen = ranks < counts[:, None]
    positions = jnp.arange(PIX_DEV)[None, :]
    order = jnp.where(chosen, positions, PIX_DEV + positions)
    picked = jnp.argsort(order, axis=1)[:, :CAP]
    picked = jnp.where(jnp.arange(CAP)[None, :] < counts[:, None], picked, 0)
    return (counts.astype(jnp.int32), picked.reshape(N_PIX * CAP).astype(jnp.int32))


def draw_clear_count(key, part):
    return clear_lists(key)[0]


def draw_clear_index(key, part):
    return clear_lists(key)[1]


def level_of(key, extent, pieces, low, high):
    factor_of, own = 1.0, jax.random.fold_in(key, 6)
    for position, parts in pieces:
        steps = jnp.exp(jax.random.uniform(jax.random.fold_in(own, position), (parts,), jnp.float32, low / len(pieces), high / len(pieces)))
        factor_of = factor_of * jnp.repeat(steps, extent[position] // parts).reshape([-1 if axis == position else 1 for axis in range(len(extent))])
    return factor_of


def gaussian(key, extent, deviation, reach, pieces=(), kind=jnp.bfloat16):
    factor_of = level_of(key, extent, pieces, -0.22, 0.18) if pieces else 1.0
    entries = jax.random.normal(key, extent, jnp.float32) * deviation * factor_of
    return jnp.minimum(jnp.maximum(entries, -reach), reach).astype(kind)


def setup_inputs(seed: int = 0) -> dict:
    seeds = jax.random.split(jax.random.key(seed), 13)
    pixels = gaussian(seeds[0], (PIXELS, SPEC, D), 1.0, 6.0, ((0, 32), (1, 16)))
    clear_count = draw_clear_count(jax.random.fold_in(seeds[12], 71), 0)
    clear_index = draw_clear_index(jax.random.fold_in(seeds[12], 71), 0)
    attn_gain = jnp.clip(1.0 + 0.18 * jax.random.normal(seeds[3], (D,), jnp.float32), 0.1, 1.9)
    w_query = draw_w_query(jax.random.fold_in(seeds[12], 71), 0)
    w_key = draw_w_key(jax.random.fold_in(seeds[12], 71), 0)
    w_value = gaussian(seeds[6], (D, HEADS * HD), D ** -0.5, 0.1875, ((1, 16),))
    w_out = gaussian(seeds[7], (HEADS * HD, D), (HEADS * HD) ** -0.5, 0.1875, ((0, 16),))
    mlp_gain = jnp.clip(1.0 + 0.18 * jax.random.normal(seeds[8], (D,), jnp.float32), 0.1, 1.9)
    w_gate = gaussian(seeds[9], (D, FF), D ** -0.5, 0.1875, ((1, 16),))
    w_up = gaussian(seeds[10], (D, FF), D ** -0.5, 0.1875, ((1, 16),))
    w_down = gaussian(seeds[11], (FF, D), FF ** -0.5, 0.09375, ((0, 16),))
    return {"pixels": pixels, "clear_count": clear_count, "clear_index": clear_index, "attn_gain": attn_gain, "w_query": w_query, "w_key": w_key, "w_value": w_value, "w_out": w_out, "mlp_gain": mlp_gain, "w_gate": w_gate, "w_up": w_up, "w_down": w_down}


def normed(rows, gain):
    full = rows.astype(jnp.float32)
    scaled = full * lax.rsqrt(lax.optimization_barrier(jnp.mean(full * full, axis=-1, keepdims=True)) + 1e-05)
    return (scaled * gain.astype(jnp.float32)).astype(jnp.bfloat16)

def reference(pixels, clear_count, clear_index, attn_gain, w_query, w_key, w_value, w_out, mlp_gain, w_gate, w_up, w_down):
    tiles = pixels.reshape(N_PIX, PIX_DEV, SPEC, D)
    slots = clear_index.reshape(N_PIX, CAP).astype(jnp.int32)
    kept = jnp.take_along_axis(tiles, slots[:, :, None, None], axis=1)
    rows = jnp.transpose(kept, (2, 0, 1, 3)).reshape(SPEC, N_PIX * CAP, D)
    live_slot = jnp.arange(CAP, dtype=jnp.int32)[None, :] < clear_count[:, None]
    live = live_slot.reshape(N_PIX * CAP)
    flat = normed(rows, attn_gain).reshape(SPEC * N_PIX * CAP, D)

    def project(weight):
        out = jnp.dot(flat, weight, preferred_element_type=jnp.float32).astype(jnp.bfloat16)
        return out.reshape(SPEC, N_PIX * CAP, HEADS, HD)
    query = project(w_query)
    key = project(w_key)
    value = project(w_value)

    def attend(block):
        q_rows, k_rows, v_rows = block
        scores = jnp.einsum('qhd,khd->hqk', q_rows.astype(jnp.float32), k_rows.astype(jnp.float32)) * HD ** (-0.5)
        masked = jnp.where(live[None, None, :], scores, -1e+30)
        top = lax.optimization_barrier(jnp.max(masked, axis=-1, keepdims=True))
        expo = jnp.where(live[None, None, :], jnp.exp(masked - top), 0.0)
        totals = lax.optimization_barrier(jnp.sum(expo, axis=-1))
        weights = expo.astype(jnp.bfloat16)
        mixed = jnp.einsum('hqk,khd->qhd', weights.astype(jnp.float32), v_rows.astype(jnp.float32))
        return (mixed / jnp.transpose(totals)[:, :, None]).astype(jnp.bfloat16)
    context = lax.map(attend, (query, key, value))
    context_groups = context.reshape(SPEC * N_PIX * CAP, N_BAND, HEADS * HD // N_BAND)
    out_groups = w_out.reshape(N_BAND, HEADS * HD // N_BAND, D)

    def add_attn(total, group):
        piece = lax.dynamic_index_in_dim(context_groups, group, 1, keepdims=False)
        weight = lax.dynamic_index_in_dim(out_groups, group, 0, keepdims=False)
        part = jnp.dot(piece, weight, preferred_element_type=jnp.float32).astype(jnp.bfloat16)
        part = lax.optimization_barrier(part)
        return (total + part.astype(jnp.float32), None)
    groups = jnp.arange(N_BAND, dtype=jnp.int32)
    attn_out, _ = lax.scan(add_attn, jnp.zeros((SPEC * N_PIX * CAP, D), jnp.float32), groups)
    state = (rows.reshape(SPEC * N_PIX * CAP, D).astype(jnp.float32) + attn_out).astype(jnp.bfloat16)
    mlp_in = normed(state, mlp_gain)
    gate_groups = w_gate.reshape(D, N_BAND, FF // N_BAND)
    up_groups = w_up.reshape(D, N_BAND, FF // N_BAND)
    down_groups = w_down.reshape(N_BAND, FF // N_BAND, D)

    def add_mlp(total, group):
        gate = jnp.dot(mlp_in, lax.dynamic_index_in_dim(gate_groups, group, 1, keepdims=False), preferred_element_type=jnp.float32)
        upper = jnp.dot(mlp_in, lax.dynamic_index_in_dim(up_groups, group, 1, keepdims=False), preferred_element_type=jnp.float32)
        hidden = (jax.nn.silu(gate) * upper).astype(jnp.bfloat16)
        part = jnp.dot(hidden, lax.dynamic_index_in_dim(down_groups, group, 0, keepdims=False), preferred_element_type=jnp.float32).astype(jnp.bfloat16)
        part = lax.optimization_barrier(part)
        return (total + part.astype(jnp.float32), None)
    mlp_out, _ = lax.scan(add_mlp, jnp.zeros((SPEC * N_PIX * CAP, D), jnp.float32), groups)
    encoded = (state.astype(jnp.float32) + mlp_out).astype(jnp.bfloat16)
    result = jnp.transpose(encoded.reshape(SPEC, N_PIX, CAP, D), (1, 2, 0, 3))
    chosen = (jnp.arange(PIX_DEV, dtype=jnp.int32)[None, :, None] == slots[:, None, :]) & live_slot[:, None, :]
    placed = jnp.einsum('tpc,tcsd->tpsd', chosen.astype(jnp.float32), result.astype(jnp.float32)).astype(jnp.bfloat16)
    taken = jnp.any(chosen, axis=2)
    return jnp.where(taken[:, :, None, None], placed, tiles).reshape(PIXELS, SPEC, D)
```

```python
import jax
import jax.numpy as jnp
from jax import lax
from jax.sharding import PartitionSpec as P

HD = 64


def normed(rows, gain):
    full = rows.astype(jnp.float32)
    scaled = full * lax.rsqrt(jnp.mean(full * full, axis=-1, keepdims=True) + 1e-05)
    return (scaled * gain).astype(jnp.bfloat16)


def band_gather(rows):
    n = lax.axis_size("band")
    sent = jnp.broadcast_to(rows[None], (n,) + rows.shape)
    got = lax.all_to_all(sent, "band", 0, 0, tiled=True)
    return got.reshape((n * rows.shape[0],) + rows.shape[1:])


def band_reduce(part):
    n = lax.axis_size("band")
    split = part.reshape((n, part.shape[0] // n) + part.shape[1:])
    got = lax.all_to_all(split, "band", 0, 0, tiled=True)
    return jnp.sum(got.astype(jnp.float32), axis=0)


def shards(
    pixels,
    clear_count,
    clear_index,
    attn_gain,
    w_query,
    w_key,
    w_value,
    w_out,
    mlp_gain,
    w_gate,
    w_up,
    w_down,
):
    own_count = clear_count[0]
    n_pix = lax.axis_size("pix")
    kept = jnp.take(pixels, clear_index, axis=0)
    kept_rows = jnp.swapaxes(kept, 0, 1)
    spec_here, slots_here, width = kept_rows.shape
    attn_in = band_gather(normed(kept_rows, attn_gain))
    spec = attn_in.shape[0]
    flat = attn_in.reshape(spec * slots_here, width)
    heads_here = w_query.shape[1] // HD

    def project(weight):
        out = jnp.dot(flat, weight, preferred_element_type=jnp.float32).astype(jnp.bfloat16)
        return out.reshape(spec, slots_here, heads_here * HD)

    live_here = jnp.arange(slots_here, dtype=jnp.int32) < own_count
    flag = jnp.broadcast_to(
        live_here.astype(jnp.bfloat16)[None, :, None], (spec, slots_here, heads_here * HD)
    )
    payload = jnp.concatenate([project(w_query), project(w_key), project(w_value), flag], axis=-1)
    mine = lax.all_to_all(payload, "pix", 0, 1, tiled=True)
    spec_mine = mine.shape[0]
    slots = mine.shape[1]
    q = mine[..., 0 * HD : heads_here * HD].reshape(spec_mine, slots, heads_here, HD)
    k = mine[..., heads_here * HD : 2 * heads_here * HD].reshape(spec_mine, slots, heads_here, HD)
    v = mine[..., 2 * heads_here * HD : 3 * heads_here * HD].reshape(spec_mine, slots, heads_here, HD)
    live = mine[0, :, 3 * heads_here * HD] > 0.5
    scores = jnp.einsum("sqhd,skhd->shqk", q, k, preferred_element_type=jnp.float32) * HD ** (-0.5)
    masked = jnp.where(live[None, None, None, :], scores, -1e30)
    top = jnp.max(masked, axis=-1)
    expo = jnp.where(live[None, None, None, :], jnp.exp(masked - top[..., None]), 0.0)
    totals = jnp.sum(expo, axis=-1)
    mixed = jnp.einsum(
        "shqk,skhd->sqhd", expo.astype(jnp.bfloat16), v, preferred_element_type=jnp.float32
    )
    context = (mixed / jnp.transpose(totals, (0, 2, 1))[..., None]).astype(jnp.bfloat16)
    context = context.reshape(spec_mine, slots, heads_here * HD)
    context_rows = lax.all_to_all(context, "pix", 1, 0, tiled=True)
    out = jnp.dot(
        context_rows.reshape(spec * slots_here, heads_here * HD),
        w_out,
        preferred_element_type=jnp.float32,
    ).astype(jnp.bfloat16)
    attn_out = band_reduce(out.reshape(spec, slots_here, width))
    state = (kept_rows.astype(jnp.float32) + attn_out).astype(jnp.bfloat16)
    mlp_in = band_gather(normed(state, mlp_gain))
    piece = mlp_in.reshape(spec * slots_here, width)
    gate = jnp.dot(piece, w_gate, preferred_element_type=jnp.float32)
    upper = jnp.dot(piece, w_up, preferred_element_type=jnp.float32)
    hidden = (jax.nn.silu(gate) * upper).astype(jnp.bfloat16)
    out = jnp.dot(hidden, w_down, preferred_element_type=jnp.float32).astype(jnp.bfloat16)
    mlp_out = band_reduce(out.reshape(spec, slots_here, width))
    encoded = (state.astype(jnp.float32) + mlp_out).astype(jnp.bfloat16)
    chosen = (
        jnp.arange(pixels.shape[0], dtype=jnp.int32)[:, None] == clear_index[None, :]
    ) & live_here[None, :]
    placed = jnp.einsum(
        "pc,scd->psd", chosen.astype(jnp.bfloat16), encoded, preferred_element_type=jnp.float32
    ).astype(jnp.bfloat16)
    taken = jnp.any(chosen, axis=1)
    return jnp.where(taken[:, None, None], placed, pixels)


def solution(mesh):
    return jax.shard_map(
        shards,
        mesh=mesh,
        in_specs=(
            P("pix", "band", None),
            P("pix"),
            P("pix"),
            P(),
            P(None, "band"),
            P(None, "band"),
            P(None, "band"),
            P("band", None),
            P(),
            P(None, "band"),
            P(None, "band"),
            P("band", None),
        ),
        out_specs=P("pix", "band", None),
        check_vma=False,
    )
```

```python
import jax
import jax.numpy as jnp
from jax import lax
from jax.sharding import Mesh, PartitionSpec as P

HD = 64


def normed(rows, gain):
    full = rows.astype(jnp.float32)
    scaled = full * lax.rsqrt(jnp.mean(full * full, axis=-1, keepdims=True) + 1e-05)
    return (scaled * gain).astype(jnp.bfloat16)


def band_gather(rows):
    n = lax.axis_size("band")
    sent = jnp.broadcast_to(rows[None], (n,) + rows.shape)
    got = lax.all_to_all(sent, "band", 0, 0, tiled=True)
    return got.reshape((n * rows.shape[0],) + rows.shape[1:])


def band_reduce(part):
    n = lax.axis_size("band")
    split = part.reshape((n, part.shape[0] // n) + part.shape[1:])
    got = lax.all_to_all(split, "band", 0, 0, tiled=True)
    return jnp.sum(got.astype(jnp.float32), axis=0)


def shards(
    pixels,
    clear_count,
    clear_index,
    attn_gain,
    w_query,
    w_key,
    w_value,
    w_out,
    mlp_gain,
    w_gate,
    w_up,
    w_down,
):
    own_count = clear_count[0]
    kept = jnp.take(pixels, clear_index, axis=0)
    kept_rows = jnp.swapaxes(kept, 0, 1)
    spec_here, slots_here, width = kept_rows.shape
    attn_in = band_gather(normed(kept_rows, attn_gain))
    spec = attn_in.shape[0]
    flat = attn_in.reshape(spec * slots_here, width)
    heads_here = w_query.shape[1] // HD

    def project(weight):
        out = jnp.dot(flat, weight, preferred_element_type=jnp.float32).astype(jnp.bfloat16)
        return out.reshape(spec, slots_here, heads_here * HD)

    live_here = jnp.arange(slots_here, dtype=jnp.int32) < own_count
    qkv = jnp.concatenate([project(w_query), project(w_key), project(w_value)], axis=-1)
    width_qkv = qkv.shape[-1]
    flag_row = jnp.zeros((spec, 1, width_qkv), jnp.bfloat16)
    flag_row = flag_row.at[:, 0, :slots_here].set(live_here.astype(jnp.bfloat16)[None, :])
    payload = jnp.concatenate([qkv, flag_row], axis=1)
    mine = lax.all_to_all(payload, "z", 0, 1, tiled=True)
    mine = lax.all_to_all(mine, "c", 0, 1, tiled=True)
    n_z, n_c = lax.axis_size("z"), lax.axis_size("c")
    spec_mine = mine.shape[0]
    mine = mine.reshape(spec_mine, n_c * n_z, slots_here + 1, width_qkv)
    live = (mine[0, :, slots_here, :slots_here] > 0.5).reshape(-1)
    rows = mine[:, :, :slots_here].reshape(spec_mine, n_c * n_z * slots_here, width_qkv)
    slots = rows.shape[1]
    q = rows[..., 0 * HD : heads_here * HD].reshape(spec_mine, slots, heads_here, HD)
    k = rows[..., heads_here * HD : 2 * heads_here * HD].reshape(spec_mine, slots, heads_here, HD)
    v = rows[..., 2 * heads_here * HD : 3 * heads_here * HD].reshape(spec_mine, slots, heads_here, HD)
    scores = jnp.einsum("sqhd,skhd->shqk", q, k, preferred_element_type=jnp.float32) * HD ** (-0.5)
    masked = jnp.where(live[None, None, None, :], scores, -1e30)
    top = jnp.max(masked, axis=-1)
    expo = jnp.where(live[None, None, None, :], jnp.exp(masked - top[..., None]), 0.0)
    totals = jnp.sum(expo, axis=-1)
    mixed = jnp.einsum(
        "shqk,skhd->sqhd", expo.astype(jnp.bfloat16), v, preferred_element_type=jnp.float32
    )
    context = (mixed / jnp.transpose(totals, (0, 2, 1))[..., None]).astype(jnp.bfloat16)
    context = context.reshape(spec_mine, n_c, n_z, slots_here, heads_here * HD)
    context = jnp.swapaxes(context, 1, 2).reshape(spec_mine, slots, heads_here * HD)
    context_rows = lax.all_to_all(context, ("z", "c"), 1, 0, tiled=True)
    out = jnp.dot(
        context_rows.reshape(spec * slots_here, heads_here * HD),
        w_out,
        preferred_element_type=jnp.float32,
    ).astype(jnp.bfloat16)
    attn_out = band_reduce(out.reshape(spec, slots_here, width))
    state = (kept_rows.astype(jnp.float32) + attn_out).astype(jnp.bfloat16)
    mlp_in = band_gather(normed(state, mlp_gain))
    piece = mlp_in.reshape(spec * slots_here, width)
    gate = jnp.dot(piece, w_gate, preferred_element_type=jnp.float32)
    upper = jnp.dot(piece, w_up, preferred_element_type=jnp.float32)
    hidden = (jax.nn.silu(gate) * upper).astype(jnp.bfloat16)
    out = jnp.dot(hidden, w_down, preferred_element_type=jnp.float32).astype(jnp.bfloat16)
    mlp_out = band_reduce(out.reshape(spec, slots_here, width))
    encoded = (state.astype(jnp.float32) + mlp_out).astype(jnp.bfloat16)
    chosen = (
        jnp.arange(pixels.shape[0], dtype=jnp.int32)[:, None] == clear_index[None, :]
    ) & live_here[None, :]
    placed = jnp.einsum(
        "pc,scd->psd", chosen.astype(jnp.bfloat16), encoded, preferred_element_type=jnp.float32
    ).astype(jnp.bfloat16)
    taken = jnp.any(chosen, axis=1)
    return jnp.where(taken[:, None, None], placed, pixels)


def solution(mesh):
    n_band, n_pix = mesh.devices.shape
    split = Mesh(mesh.devices.reshape(n_band, n_pix // 2, 2), ("band", "z", "c"))
    pix = ("z", "c")
    return jax.shard_map(
        shards,
        mesh=split,
        in_specs=(
            P(pix, "band", None),
            P(pix),
            P(pix),
            P(),
            P(None, "band"),
            P(None, "band"),
            P(None, "band"),
            P("band", None),
            P(),
            P(None, "band"),
            P(None, "band"),
            P("band", None),
        ),
        out_specs=P(pix, "band", None),
        check_vma=False,
    )
```

```python
import jax
import jax.numpy as jnp
from jax import lax
from jax.sharding import Mesh, PartitionSpec as P

HD = 64


def normed(rows, gain):
    full = rows.astype(jnp.float32)
    scaled = full * lax.rsqrt(jnp.mean(full * full, axis=-1, keepdims=True) + 1e-05)
    return (scaled * gain).astype(jnp.bfloat16)


def band_gather(rows):
    n = lax.axis_size("band")
    sent = jnp.broadcast_to(rows[None], (n,) + rows.shape)
    got = lax.all_to_all(sent, "band", 0, 0, tiled=True)
    return got.reshape((n * rows.shape[0],) + rows.shape[1:])


def band_reduce(part):
    n = lax.axis_size("band")
    split = part.reshape((n, part.shape[0] // n) + part.shape[1:])
    got = lax.all_to_all(split, "band", 0, 0, tiled=True)
    return jnp.sum(got.astype(jnp.float32), axis=0)


def shards(
    pixels,
    clear_count,
    clear_index,
    attn_gain,
    w_query,
    w_key,
    w_value,
    w_out,
    mlp_gain,
    w_gate,
    w_up,
    w_down,
):
    own_count = clear_count[0]
    kept = jnp.take(pixels, clear_index, axis=0)
    kept_rows = jnp.swapaxes(kept, 0, 1)
    spec_here, slots_here, width = kept_rows.shape
    w_out_all = lax.all_gather(w_out, "band", axis=0, tiled=True)
    kept_all = band_gather(kept_rows)
    attn_in = normed(kept_all, attn_gain)
    spec = attn_in.shape[0]
    flat = attn_in.reshape(spec * slots_here, width)
    heads_here = w_query.shape[1] // HD

    def project(weight):
        out = jnp.dot(flat, weight, preferred_element_type=jnp.float32).astype(jnp.bfloat16)
        return out.reshape(spec, slots_here, heads_here * HD)

    live_here = jnp.arange(slots_here, dtype=jnp.int32) < own_count
    qkv = jnp.concatenate([project(w_query), project(w_key), project(w_value)], axis=-1)
    width_qkv = qkv.shape[-1]
    flag_row = jnp.zeros((spec, 1, width_qkv), jnp.bfloat16)
    flag_row = flag_row.at[:, 0, :slots_here].set(live_here.astype(jnp.bfloat16)[None, :])
    payload = jnp.concatenate([qkv, flag_row], axis=1)
    mine = lax.all_to_all(payload, "z", 0, 1, tiled=True)
    mine = lax.all_to_all(mine, "c", 0, 1, tiled=True)
    n_z, n_c = lax.axis_size("z"), lax.axis_size("c")
    spec_mine = mine.shape[0]
    mine = mine.reshape(spec_mine, n_c * n_z, slots_here + 1, width_qkv)
    live = (mine[0, :, slots_here, :slots_here] > 0.5).reshape(-1)
    rows = mine[:, :, :slots_here].reshape(spec_mine, n_c * n_z * slots_here, width_qkv)
    slots = rows.shape[1]
    q = rows[..., 0 * HD : heads_here * HD].reshape(spec_mine, slots, heads_here, HD)
    k = rows[..., heads_here * HD : 2 * heads_here * HD].reshape(spec_mine, slots, heads_here, HD)
    v = rows[..., 2 * heads_here * HD : 3 * heads_here * HD].reshape(spec_mine, slots, heads_here, HD)
    scores = jnp.einsum("sqhd,skhd->shqk", q, k, preferred_element_type=jnp.float32) * HD ** (-0.5)
    masked = jnp.where(live[None, None, None, :], scores, -1e30)
    top = jnp.max(masked, axis=-1)
    expo = jnp.where(live[None, None, None, :], jnp.exp(masked - top[..., None]), 0.0)
    totals = jnp.sum(expo, axis=-1)
    mixed = jnp.einsum(
        "shqk,skhd->sqhd", expo.astype(jnp.bfloat16), v, preferred_element_type=jnp.float32
    )
    context = (mixed / jnp.transpose(totals, (0, 2, 1))[..., None]).astype(jnp.bfloat16)
    context = context.reshape(spec_mine, n_c, n_z, slots_here, heads_here * HD)
    context = jnp.swapaxes(context, 1, 2).reshape(spec_mine, slots, heads_here * HD)
    context_rows = lax.all_to_all(context, ("z", "c"), 1, 0, tiled=True)
    n_band = lax.axis_size("band")
    sent = jnp.broadcast_to(context_rows[None], (n_band,) + context_rows.shape)
    context_all = lax.all_to_all(sent, "band", 0, 0, tiled=True)
    context_all = jnp.transpose(context_all, (1, 2, 0, 3)).reshape(spec * slots_here, width)
    attn_out = jnp.dot(context_all, w_out_all, preferred_element_type=jnp.float32)
    state_all = (kept_all.reshape(spec * slots_here, width).astype(jnp.float32) + attn_out).astype(jnp.bfloat16)
    mlp_in = normed(state_all, mlp_gain)
    band = lax.axis_index("band")
    state = lax.dynamic_slice_in_dim(state_all.reshape(spec, slots_here, width), band * spec_here, spec_here, 0)
    piece = mlp_in.reshape(spec * slots_here, width)
    gate = jnp.dot(piece, w_gate, preferred_element_type=jnp.float32)
    upper = jnp.dot(piece, w_up, preferred_element_type=jnp.float32)
    hidden = (jax.nn.silu(gate) * upper).astype(jnp.bfloat16)
    out = jnp.dot(hidden, w_down, preferred_element_type=jnp.float32).astype(jnp.bfloat16)
    mlp_out = band_reduce(out.reshape(spec, slots_here, width))
    encoded = (state.astype(jnp.float32) + mlp_out).astype(jnp.bfloat16)
    chosen = (
        jnp.arange(pixels.shape[0], dtype=jnp.int32)[:, None] == clear_index[None, :]
    ) & live_here[None, :]
    placed = jnp.einsum(
        "pc,scd->psd", chosen.astype(jnp.bfloat16), encoded, preferred_element_type=jnp.float32
    ).astype(jnp.bfloat16)
    taken = jnp.any(chosen, axis=1)
    return jnp.where(taken[:, None, None], placed, pixels)


def solution(mesh):
    n_band, n_pix = mesh.devices.shape
    split = Mesh(mesh.devices.reshape(n_band, n_pix // 2, 2), ("band", "z", "c"))
    pix = ("z", "c")
    return jax.shard_map(
        shards,
        mesh=split,
        in_specs=(
            P(pix, "band", None),
            P(pix),
            P(pix),
            P(),
            P(None, "band"),
            P(None, "band"),
            P(None, "band"),
            P("band", None),
            P(),
            P(None, "band"),
            P(None, "band"),
            P("band", None),
        ),
        out_specs=P(pix, "band", None),
        check_vma=False,
    )
```

```python
import jax
import jax.numpy as jnp
from jax import lax
from jax.sharding import Mesh, PartitionSpec as P

HD = 64


def normed(rows, gain):
    full = rows.astype(jnp.float32)
    scaled = full * lax.rsqrt(jnp.mean(full * full, axis=-1, keepdims=True) + 1e-05)
    return (scaled * gain).astype(jnp.bfloat16)


def band_gather(rows):
    n = lax.axis_size("band")
    sent = jnp.broadcast_to(rows[None], (n,) + rows.shape)
    got = lax.all_to_all(sent, "band", 0, 0, tiled=True)
    return got.reshape((n * rows.shape[0],) + rows.shape[1:])


def band_reduce(part):
    n = lax.axis_size("band")
    split = part.reshape((n, part.shape[0] // n) + part.shape[1:])
    got = lax.all_to_all(split, "band", 0, 0, tiled=True)
    return jnp.sum(got.astype(jnp.float32), axis=0)


def shards(
    pixels,
    clear_count,
    clear_index,
    attn_gain,
    w_query,
    w_key,
    w_value,
    w_out,
    mlp_gain,
    w_gate,
    w_up,
    w_down,
):
    own_count = clear_count[0]
    kept = jnp.take(pixels, clear_index, axis=0)
    kept_rows = jnp.swapaxes(kept, 0, 1)
    spec_here, slots_here, width = kept_rows.shape
    n_band = lax.axis_size("band")
    both = jnp.concatenate([kept_rows.reshape(spec_here * slots_here, width), w_out], axis=0)
    both = lax.all_to_all(jnp.broadcast_to(both[None], (n_band,) + both.shape), "band", 0, 0, tiled=True)
    kept_all = both[:, : spec_here * slots_here].reshape(n_band * spec_here, slots_here, width)
    w_out_all = both[:, spec_here * slots_here :].reshape(n_band * w_out.shape[0], width)
    attn_in = normed(kept_all, attn_gain)
    spec = attn_in.shape[0]
    flat = attn_in.reshape(spec * slots_here, width)
    heads_here = w_query.shape[1] // HD

    def project(weight):
        out = jnp.dot(flat, weight, preferred_element_type=jnp.float32).astype(jnp.bfloat16)
        return out.reshape(spec, slots_here, heads_here * HD)

    live_here = jnp.arange(slots_here, dtype=jnp.int32) < own_count
    qkv = jnp.concatenate([project(w_query), project(w_key), project(w_value)], axis=-1)
    width_qkv = qkv.shape[-1]
    flag_row = jnp.zeros((spec, 1, width_qkv), jnp.bfloat16)
    flag_row = flag_row.at[:, 0, :slots_here].set(live_here.astype(jnp.bfloat16)[None, :])
    payload = jnp.concatenate([qkv, flag_row], axis=1)
    mine = lax.all_to_all(payload, "z", 0, 1, tiled=True)
    mine = lax.all_to_all(mine, "c", 0, 1, tiled=True)
    n_z, n_c = lax.axis_size("z"), lax.axis_size("c")
    spec_mine = mine.shape[0]
    mine = mine.reshape(spec_mine, n_c * n_z, slots_here + 1, width_qkv)
    live = (mine[0, :, slots_here, :slots_here] > 0.5).reshape(-1)
    rows = mine[:, :, :slots_here].reshape(spec_mine, n_c * n_z * slots_here, width_qkv)
    slots = rows.shape[1]
    q = rows[..., 0 * HD : heads_here * HD].reshape(spec_mine, slots, heads_here, HD)
    k = rows[..., heads_here * HD : 2 * heads_here * HD].reshape(spec_mine, slots, heads_here, HD)
    v = rows[..., 2 * heads_here * HD : 3 * heads_here * HD].reshape(spec_mine, slots, heads_here, HD)
    scores = jnp.einsum("sqhd,skhd->shqk", q, k, preferred_element_type=jnp.float32) * HD ** (-0.5)
    masked = jnp.where(live[None, None, None, :], scores, -1e30)
    top = jnp.max(masked, axis=-1)
    expo = jnp.where(live[None, None, None, :], jnp.exp(masked - top[..., None]), 0.0)
    totals = jnp.sum(expo, axis=-1)
    mixed = jnp.einsum(
        "shqk,skhd->sqhd", expo.astype(jnp.bfloat16), v, preferred_element_type=jnp.float32
    )
    context = (mixed / jnp.transpose(totals, (0, 2, 1))[..., None]).astype(jnp.bfloat16)
    context = context.reshape(spec_mine, n_c, n_z, slots_here, heads_here * HD)
    context = jnp.swapaxes(context, 1, 2).reshape(spec_mine, slots, heads_here * HD)
    context_rows = lax.all_to_all(context, ("z", "c"), 1, 0, tiled=True)
    sent = jnp.broadcast_to(context_rows[None], (n_band,) + context_rows.shape)
    context_all = lax.all_to_all(sent, "band", 0, 0, tiled=True)
    context_all = jnp.transpose(context_all, (1, 2, 0, 3)).reshape(spec * slots_here, width)
    attn_out = jnp.dot(context_all, w_out_all, preferred_element_type=jnp.float32)
    state_all = (kept_all.reshape(spec * slots_here, width).astype(jnp.float32) + attn_out).astype(jnp.bfloat16)
    mlp_in = normed(state_all, mlp_gain)
    band = lax.axis_index("band")
    state = lax.dynamic_slice_in_dim(state_all.reshape(spec, slots_here, width), band * spec_here, spec_here, 0)
    piece = mlp_in.reshape(spec * slots_here, width)
    gate = jnp.dot(piece, w_gate, preferred_element_type=jnp.float32)
    upper = jnp.dot(piece, w_up, preferred_element_type=jnp.float32)
    hidden = (jax.nn.silu(gate) * upper).astype(jnp.bfloat16)
    out = jnp.dot(hidden, w_down, preferred_element_type=jnp.float32).astype(jnp.bfloat16)
    mlp_out = band_reduce(out.reshape(spec, slots_here, width))
    encoded = (state.astype(jnp.float32) + mlp_out).astype(jnp.bfloat16)
    chosen = (
        jnp.arange(pixels.shape[0], dtype=jnp.int32)[:, None] == clear_index[None, :]
    ) & live_here[None, :]
    placed = jnp.einsum(
        "pc,scd->psd", chosen.astype(jnp.bfloat16), encoded, preferred_element_type=jnp.float32
    ).astype(jnp.bfloat16)
    taken = jnp.any(chosen, axis=1)
    return jnp.where(taken[:, None, None], placed, pixels)


def solution(mesh):
    n_band, n_pix = mesh.devices.shape
    split = Mesh(mesh.devices.reshape(n_band, n_pix // 2, 2), ("band", "z", "c"))
    pix = ("z", "c")
    return jax.shard_map(
        shards,
        mesh=split,
        in_specs=(
            P(pix, "band", None),
            P(pix),
            P(pix),
            P(),
            P(None, "band"),
            P(None, "band"),
            P(None, "band"),
            P("band", None),
            P(),
            P(None, "band"),
            P(None, "band"),
            P("band", None),
        ),
        out_specs=P(pix, "band", None),
        check_vma=False,
    )
```

```python
import jax
import jax.numpy as jnp
from jax import lax
from jax.sharding import Mesh, PartitionSpec as P

HD = 64


def normed(rows, gain):
    full = rows.astype(jnp.float32)
    scaled = full * lax.rsqrt(jnp.mean(full * full, axis=-1, keepdims=True) + 1e-05)
    return (scaled * gain).astype(jnp.bfloat16)


def band_gather(rows):
    n = lax.axis_size("band")
    sent = jnp.broadcast_to(rows[None], (n,) + rows.shape)
    got = lax.all_to_all(sent, "band", 0, 0, tiled=True)
    return got.reshape((n * rows.shape[0],) + rows.shape[1:])


def band_reduce(part):
    n = lax.axis_size("band")
    split = part.reshape((n, part.shape[0] // n) + part.shape[1:])
    got = lax.all_to_all(split, "band", 0, 0, tiled=True)
    return jnp.sum(got.astype(jnp.float32), axis=0)


def shards(
    pixels,
    clear_count,
    clear_index,
    attn_gain,
    w_query,
    w_key,
    w_value,
    w_out,
    mlp_gain,
    w_gate,
    w_up,
    w_down,
):
    own_count = clear_count[0]
    kept = jnp.take(pixels, clear_index, axis=0)
    kept_rows = jnp.swapaxes(kept, 0, 1)
    spec_here, slots_here, width = kept_rows.shape
    attn_in = band_gather(normed(kept_rows, attn_gain))
    spec = attn_in.shape[0]
    flat = attn_in.reshape(spec * slots_here, width)
    heads_here = w_query.shape[1] // HD

    def project(weight):
        out = jnp.dot(flat, weight, preferred_element_type=jnp.float32).astype(jnp.bfloat16)
        return out.reshape(spec, slots_here, heads_here * HD)

    live_here = jnp.arange(slots_here, dtype=jnp.int32) < own_count
    qkv = jnp.concatenate([project(w_query), project(w_key), project(w_value)], axis=-1)
    width_qkv = qkv.shape[-1]
    flag_row = jnp.zeros((spec, 1, width_qkv), jnp.bfloat16)
    at = heads_here * HD
    flag_row = flag_row.at[:, 0, at : at + slots_here].set(live_here.astype(jnp.bfloat16)[None, :])
    payload = jnp.concatenate([qkv, flag_row], axis=1)
    mine = lax.all_to_all(payload, "z", 0, 1, tiled=True)
    n_z = lax.axis_size("z")
    spec_mine = mine.shape[0]
    mine = mine.reshape(spec_mine, n_z, slots_here + 1, width_qkv)
    kv_flag = mine[..., heads_here * HD :]
    other = lax.ppermute(kv_flag, "c", [(0, 1), (1, 0)])
    kv_flag = jnp.concatenate([kv_flag, other], axis=1)
    live = (kv_flag[0, :, slots_here, :slots_here] > 0.5).reshape(-1)
    kv = kv_flag[:, :, :slots_here].reshape(spec_mine, -1, 2 * heads_here * HD)
    q_slots = n_z * slots_here
    q = mine[:, :, :slots_here, : heads_here * HD].reshape(spec_mine, q_slots, heads_here, HD)
    k = kv[..., : heads_here * HD].reshape(spec_mine, -1, heads_here, HD)
    v = kv[..., heads_here * HD :].reshape(spec_mine, -1, heads_here, HD)
    scores = jnp.einsum("sqhd,skhd->shqk", q, k, preferred_element_type=jnp.float32) * HD ** (-0.5)
    masked = jnp.where(live[None, None, None, :], scores, -1e30)
    top = jnp.max(masked, axis=-1)
    expo = jnp.where(live[None, None, None, :], jnp.exp(masked - top[..., None]), 0.0)
    totals = jnp.sum(expo, axis=-1)
    mixed = jnp.einsum(
        "shqk,skhd->sqhd", expo.astype(jnp.bfloat16), v, preferred_element_type=jnp.float32
    )
    context = (mixed / jnp.transpose(totals, (0, 2, 1))[..., None]).astype(jnp.bfloat16)
    context = context.reshape(spec_mine, q_slots, heads_here * HD)
    context_rows = lax.all_to_all(context, "z", 1, 0, tiled=True)
    out = jnp.dot(
        context_rows.reshape(spec * slots_here, heads_here * HD),
        w_out,
        preferred_element_type=jnp.float32,
    ).astype(jnp.bfloat16)
    attn_out = band_reduce(out.reshape(spec, slots_here, width))
    state = (kept_rows.astype(jnp.float32) + attn_out).astype(jnp.bfloat16)
    mlp_in = band_gather(normed(state, mlp_gain))
    piece = mlp_in.reshape(spec * slots_here, width)
    gate = jnp.dot(piece, w_gate, preferred_element_type=jnp.float32)
    upper = jnp.dot(piece, w_up, preferred_element_type=jnp.float32)
    hidden = (jax.nn.silu(gate) * upper).astype(jnp.bfloat16)
    out = jnp.dot(hidden, w_down, preferred_element_type=jnp.float32).astype(jnp.bfloat16)
    mlp_out = band_reduce(out.reshape(spec, slots_here, width))
    encoded = (state.astype(jnp.float32) + mlp_out).astype(jnp.bfloat16)
    chosen = (
        jnp.arange(pixels.shape[0], dtype=jnp.int32)[:, None] == clear_index[None, :]
    ) & live_here[None, :]
    placed = jnp.einsum(
        "pc,scd->psd", chosen.astype(jnp.bfloat16), encoded, preferred_element_type=jnp.float32
    ).astype(jnp.bfloat16)
    taken = jnp.any(chosen, axis=1)
    return jnp.where(taken[:, None, None], placed, pixels)


def solution(mesh):
    n_band, n_pix = mesh.devices.shape
    split = Mesh(mesh.devices.reshape(n_band, n_pix // 2, 2), ("band", "z", "c"))
    pix = ("z", "c")
    return jax.shard_map(
        shards,
        mesh=split,
        in_specs=(
            P(pix, "band", None),
            P(pix),
            P(pix),
            P(),
            P(None, "band"),
            P(None, "band"),
            P(None, "band"),
            P("band", None),
            P(),
            P(None, "band"),
            P(None, "band"),
            P("band", None),
        ),
        out_specs=P(pix, "band", None),
        check_vma=False,
    )
```

```python
import jax
import jax.numpy as jnp
from jax import lax
from jax.sharding import Mesh, PartitionSpec as P

HD = 64


def normed(rows, gain):
    full = rows.astype(jnp.float32)
    scaled = full * lax.rsqrt(jnp.mean(full * full, axis=-1, keepdims=True) + 1e-05)
    return (scaled * gain).astype(jnp.bfloat16)


def band_gather(rows):
    n = lax.axis_size("band")
    sent = jnp.broadcast_to(rows[None], (n,) + rows.shape)
    got = lax.all_to_all(sent, "band", 0, 0, tiled=True)
    return got.reshape((n * rows.shape[0],) + rows.shape[1:])


def band_reduce(part):
    n = lax.axis_size("band")
    split = part.reshape((n, part.shape[0] // n) + part.shape[1:])
    got = lax.all_to_all(split, "band", 0, 0, tiled=True)
    return jnp.sum(got.astype(jnp.float32), axis=0)


def shards(
    pixels,
    clear_count,
    clear_index,
    attn_gain,
    w_query,
    w_key,
    w_value,
    w_out,
    mlp_gain,
    w_gate,
    w_up,
    w_down,
):
    own_count = clear_count[0]
    kept = jnp.take(pixels, clear_index, axis=0)
    kept_rows = jnp.swapaxes(kept, 0, 1)
    spec_here, slots_here, width = kept_rows.shape
    attn_in = band_gather(normed(kept_rows, attn_gain))
    spec = attn_in.shape[0]
    flat = attn_in.reshape(spec * slots_here, width)
    heads_here = w_query.shape[1] // HD

    def project(weight):
        out = jnp.dot(flat, weight, preferred_element_type=jnp.float32).astype(jnp.bfloat16)
        return out.reshape(spec, slots_here, heads_here * HD)

    live_here = jnp.arange(slots_here, dtype=jnp.int32) < own_count
    qkv = jnp.concatenate([project(w_query), project(w_key), project(w_value)], axis=-1)
    width_qkv = qkv.shape[-1]
    flag_row = jnp.zeros((spec, 1, width_qkv), jnp.bfloat16)
    at = heads_here * HD
    flag_row = flag_row.at[:, 0, at : at + slots_here].set(live_here.astype(jnp.bfloat16)[None, :])
    payload = jnp.concatenate([qkv, flag_row], axis=1)
    n_z = lax.axis_size("z")
    spec_mine = spec // n_z
    mine = lax.all_to_all(payload.reshape(n_z, -1), "z", 0, 0, tiled=True)
    mine = mine.reshape(n_z, spec_mine, slots_here + 1, width_qkv)
    mine = jnp.swapaxes(mine, 0, 1)
    kv_flag = mine[..., heads_here * HD :]
    other = lax.ppermute(kv_flag, "c", [(0, 1), (1, 0)])
    kv_flag = jnp.concatenate([kv_flag, other], axis=1)
    live = (kv_flag[0, :, slots_here, :slots_here] > 0.5).reshape(-1)
    kv = kv_flag[:, :, :slots_here].reshape(spec_mine, -1, 2 * heads_here * HD)
    q_slots = n_z * slots_here
    q = mine[:, :, :slots_here, : heads_here * HD].reshape(spec_mine, q_slots, heads_here, HD)
    k = kv[..., : heads_here * HD].reshape(spec_mine, -1, heads_here, HD)
    v = kv[..., heads_here * HD :].reshape(spec_mine, -1, heads_here, HD)
    scores = jnp.einsum("sqhd,skhd->shqk", q, k, preferred_element_type=jnp.float32) * HD ** (-0.5)
    masked = jnp.where(live[None, None, None, :], scores, -1e30)
    top = jnp.max(masked, axis=-1)
    expo = jnp.where(live[None, None, None, :], jnp.exp(masked - top[..., None]), 0.0)
    totals = jnp.sum(expo, axis=-1)
    mixed = jnp.einsum(
        "shqk,skhd->sqhd", expo.astype(jnp.bfloat16), v, preferred_element_type=jnp.float32
    )
    context = (mixed / jnp.transpose(totals, (0, 2, 1))[..., None]).astype(jnp.bfloat16)
    context = context.reshape(spec_mine, q_slots, heads_here * HD)
    context = jnp.swapaxes(context.reshape(spec_mine, n_z, -1), 0, 1).reshape(n_z, -1)
    context_rows = lax.all_to_all(context, "z", 0, 0, tiled=True)
    context_rows = context_rows.reshape(spec, slots_here, heads_here * HD)
    out = jnp.dot(
        context_rows.reshape(spec * slots_here, heads_here * HD),
        w_out,
        preferred_element_type=jnp.float32,
    ).astype(jnp.bfloat16)
    attn_out = band_reduce(out.reshape(spec, slots_here, width))
    state = (kept_rows.astype(jnp.float32) + attn_out).astype(jnp.bfloat16)
    mlp_in = band_gather(normed(state, mlp_gain))
    piece = mlp_in.reshape(spec * slots_here, width)
    gate = jnp.dot(piece, w_gate, preferred_element_type=jnp.float32)
    upper = jnp.dot(piece, w_up, preferred_element_type=jnp.float32)
    hidden = (jax.nn.silu(gate) * upper).astype(jnp.bfloat16)
    out = jnp.dot(hidden, w_down, preferred_element_type=jnp.float32).astype(jnp.bfloat16)
    mlp_out = band_reduce(out.reshape(spec, slots_here, width))
    encoded = (state.astype(jnp.float32) + mlp_out).astype(jnp.bfloat16)
    chosen = (
        jnp.arange(pixels.shape[0], dtype=jnp.int32)[:, None] == clear_index[None, :]
    ) & live_here[None, :]
    placed = jnp.einsum(
        "pc,scd->psd", chosen.astype(jnp.bfloat16), encoded, preferred_element_type=jnp.float32
    ).astype(jnp.bfloat16)
    taken = jnp.any(chosen, axis=1)
    return jnp.where(taken[:, None, None], placed, pixels)


def solution(mesh):
    n_band, n_pix = mesh.devices.shape
    split = Mesh(mesh.devices.reshape(n_band, n_pix // 2, 2), ("band", "z", "c"))
    pix = ("z", "c")
    return jax.shard_map(
        shards,
        mesh=split,
        in_specs=(
            P(pix, "band", None),
            P(pix),
            P(pix),
            P(),
            P(None, "band"),
            P(None, "band"),
            P(None, "band"),
            P("band", None),
            P(),
            P(None, "band"),
            P(None, "band"),
            P("band", None),
        ),
        out_specs=P(pix, "band", None),
        check_vma=False,
    )
```

```python
import jax
import jax.numpy as jnp
from jax import lax
from jax.sharding import Mesh, PartitionSpec as P

HD = 64


def normed(rows, gain):
    full = rows.astype(jnp.float32)
    scaled = full * lax.rsqrt(jnp.mean(full * full, axis=-1, keepdims=True) + 1e-05)
    return (scaled * gain).astype(jnp.bfloat16)


def band_gather(rows):
    n = lax.axis_size("band")
    sent = jnp.broadcast_to(rows[None], (n,) + rows.shape)
    got = lax.all_to_all(sent, "band", 0, 0, tiled=True)
    return got.reshape((n * rows.shape[0],) + rows.shape[1:])


def band_reduce(part):
    n = lax.axis_size("band")
    split = part.reshape((n, part.shape[0] // n) + part.shape[1:])
    got = lax.all_to_all(split, "band", 0, 0, tiled=True)
    return jnp.sum(got.astype(jnp.float32), axis=0)


def shards(
    pixels,
    clear_count,
    clear_index,
    attn_gain,
    w_query,
    w_key,
    w_value,
    w_out,
    mlp_gain,
    w_gate,
    w_up,
    w_down,
):
    own_count = clear_count[0]
    kept = jnp.take(pixels, clear_index, axis=0)
    kept_rows = jnp.swapaxes(kept, 0, 1)
    spec_here, slots_here, width = kept_rows.shape
    n_sq = lax.axis_size("band")
    assert n_sq == lax.axis_size("z")
    transpose = [(b * n_sq + z, z * n_sq + b) for b in range(n_sq) for z in range(n_sq)]
    kept_t = lax.ppermute(kept_rows, ("band", "z"), transpose)
    attn_in = band_gather(normed(kept_rows, attn_gain))
    spec = attn_in.shape[0]
    flat = attn_in.reshape(spec * slots_here, width)
    heads_here = w_query.shape[1] // HD

    def project(weight):
        out = jnp.dot(flat, weight, preferred_element_type=jnp.float32).astype(jnp.bfloat16)
        return out.reshape(spec, slots_here, heads_here * HD)

    live_here = jnp.arange(slots_here, dtype=jnp.int32) < own_count
    qkv = jnp.concatenate([project(w_query), project(w_key), project(w_value)], axis=-1)
    width_qkv = qkv.shape[-1]
    flag_row = jnp.zeros((spec, 1, width_qkv), jnp.bfloat16)
    at = heads_here * HD
    flag_row = flag_row.at[:, 0, at : at + slots_here].set(live_here.astype(jnp.bfloat16)[None, :])
    payload = jnp.concatenate([qkv, flag_row], axis=1)
    n_z = lax.axis_size("z")
    spec_mine = spec // n_z
    mine = lax.all_to_all(payload.reshape(n_z, -1), "z", 0, 0, tiled=True)
    mine = mine.reshape(n_z, spec_mine, slots_here + 1, width_qkv)
    mine = jnp.swapaxes(mine, 0, 1)
    kv_flag = mine[..., heads_here * HD :]
    other = lax.ppermute(kv_flag, "c", [(0, 1), (1, 0)])
    kv_flag = jnp.concatenate([kv_flag, other], axis=1)
    live = (kv_flag[0, :, slots_here, :slots_here] > 0.5).reshape(-1)
    kv = kv_flag[:, :, :slots_here].reshape(spec_mine, -1, 2 * heads_here * HD)
    q_slots = n_z * slots_here
    q = mine[:, :, :slots_here, : heads_here * HD].reshape(spec_mine, q_slots, heads_here, HD)
    k = kv[..., : heads_here * HD].reshape(spec_mine, -1, heads_here, HD)
    v = kv[..., heads_here * HD :].reshape(spec_mine, -1, heads_here, HD)
    scores = jnp.einsum("sqhd,skhd->shqk", q, k, preferred_element_type=jnp.float32) * HD ** (-0.5)
    masked = jnp.where(live[None, None, None, :], scores, -1e30)
    top = jnp.max(masked, axis=-1)
    expo = jnp.where(live[None, None, None, :], jnp.exp(masked - top[..., None]), 0.0)
    totals = jnp.sum(expo, axis=-1)
    mixed = jnp.einsum(
        "shqk,skhd->sqhd", expo.astype(jnp.bfloat16), v, preferred_element_type=jnp.float32
    )
    context = (mixed / jnp.transpose(totals, (0, 2, 1))[..., None]).astype(jnp.bfloat16)
    out = jnp.dot(
        context.reshape(spec_mine * q_slots, heads_here * HD), w_out, preferred_element_type=jnp.float32
    ).astype(jnp.bfloat16)
    out = jnp.swapaxes(out.reshape(spec_mine, n_z, slots_here, width), 0, 1)
    attn_out = band_reduce(out.reshape(n_z * spec_mine, slots_here, width))
    state = (kept_t.astype(jnp.float32) + attn_out).astype(jnp.bfloat16)
    mlp_in = band_gather(normed(state, mlp_gain))
    piece = mlp_in.reshape(-1, width)
    gate = jnp.dot(piece, w_gate, preferred_element_type=jnp.float32)
    upper = jnp.dot(piece, w_up, preferred_element_type=jnp.float32)
    hidden = (jax.nn.silu(gate) * upper).astype(jnp.bfloat16)
    out = jnp.dot(hidden, w_down, preferred_element_type=jnp.float32).astype(jnp.bfloat16)
    mlp_out = band_reduce(out.reshape(mlp_in.shape))
    encoded_t = (state.astype(jnp.float32) + mlp_out).astype(jnp.bfloat16)
    encoded = lax.ppermute(encoded_t, ("band", "z"), transpose)
    chosen = (
        jnp.arange(pixels.shape[0], dtype=jnp.int32)[:, None] == clear_index[None, :]
    ) & live_here[None, :]
    placed = jnp.einsum(
        "pc,scd->psd", chosen.astype(jnp.bfloat16), encoded, preferred_element_type=jnp.float32
    ).astype(jnp.bfloat16)
    taken = jnp.any(chosen, axis=1)
    return jnp.where(taken[:, None, None], placed, pixels)


def solution(mesh):
    n_band, n_pix = mesh.devices.shape
    split = Mesh(mesh.devices.reshape(n_band, n_pix // 2, 2), ("band", "z", "c"))
    pix = ("z", "c")
    return jax.shard_map(
        shards,
        mesh=split,
        in_specs=(
            P(pix, "band", None),
            P(pix),
            P(pix),
            P(),
            P(None, "band"),
            P(None, "band"),
            P(None, "band"),
            P("band", None),
            P(),
            P(None, "band"),
            P(None, "band"),
            P("band", None),
        ),
        out_specs=P(pix, "band", None),
        check_vma=False,
    )
```

```python
import jax
import jax.numpy as jnp
from jax import lax
from jax.sharding import Mesh, PartitionSpec as P

HD = 64


def normed(rows, gain):
    full = rows.astype(jnp.float32)
    scaled = full * lax.rsqrt(jnp.mean(full * full, axis=-1, keepdims=True) + 1e-05)
    return (scaled * gain).astype(jnp.bfloat16)


def band_gather(rows):
    n = lax.axis_size("band")
    sent = jnp.broadcast_to(rows[None], (n,) + rows.shape)
    got = lax.all_to_all(sent, "band", 0, 0, tiled=True)
    return got.reshape((n * rows.shape[0],) + rows.shape[1:])


def band_reduce(part):
    n = lax.axis_size("band")
    split = part.reshape((n, part.shape[0] // n) + part.shape[1:])
    got = lax.all_to_all(split, "band", 0, 0, tiled=True)
    return jnp.sum(got.astype(jnp.float32), axis=0)


def band_sum(part):
    got = lax.all_to_all(jnp.swapaxes(part, 1, 2), "band", 0, 0, tiled=True)
    return jnp.sum(got.astype(jnp.float32), axis=0)


def shards(
    pixels,
    clear_count,
    clear_index,
    attn_gain,
    w_query,
    w_key,
    w_value,
    w_out,
    mlp_gain,
    w_gate,
    w_up,
    w_down,
):
    own_count = clear_count[0]
    kept = jnp.take(pixels, clear_index, axis=0)
    kept_rows = jnp.swapaxes(kept, 0, 1)
    spec_here, slots_here, width = kept_rows.shape
    attn_in = band_gather(normed(kept_rows, attn_gain))
    spec = attn_in.shape[0]
    flat = attn_in.reshape(spec * slots_here, width)
    heads_here = w_query.shape[1] // HD

    def project(weight):
        out = jnp.dot(flat, weight, preferred_element_type=jnp.float32).astype(jnp.bfloat16)
        return out.reshape(spec, slots_here, heads_here * HD)

    live_here = jnp.arange(slots_here, dtype=jnp.int32) < own_count
    qkv = jnp.concatenate([project(w_query), project(w_key), project(w_value)], axis=-1)
    width_qkv = qkv.shape[-1]
    flag_row = jnp.zeros((spec, 1, width_qkv), jnp.bfloat16)
    at = heads_here * HD
    flag_row = flag_row.at[:, 0, at : at + slots_here].set(live_here.astype(jnp.bfloat16)[None, :])
    payload = jnp.concatenate([qkv, flag_row], axis=1)
    n_z = lax.axis_size("z")
    spec_mine = spec // n_z
    mine = lax.all_to_all(payload.reshape(n_z, -1), "z", 0, 0, tiled=True)
    mine = mine.reshape(n_z, spec_mine, slots_here + 1, width_qkv)
    mine = jnp.swapaxes(mine, 0, 1)
    kv_flag = mine[..., heads_here * HD :]
    other = lax.ppermute(kv_flag, "c", [(0, 1), (1, 0)])
    kv_flag = jnp.concatenate([kv_flag, other], axis=1)
    live = (kv_flag[0, :, slots_here, :slots_here] > 0.5).reshape(-1)
    kv = kv_flag[:, :, :slots_here].reshape(spec_mine, -1, 2 * heads_here * HD)
    q_slots = n_z * slots_here
    q = mine[:, :, :slots_here, : heads_here * HD].reshape(spec_mine, q_slots, heads_here, HD)
    k = kv[..., : heads_here * HD].reshape(spec_mine, -1, heads_here, HD)
    v = kv[..., heads_here * HD :].reshape(spec_mine, -1, heads_here, HD)
    scores = jnp.einsum("sqhd,skhd->shqk", q, k, preferred_element_type=jnp.float32) * HD ** (-0.5)
    masked = jnp.where(live[None, None, None, :], scores, -1e30)
    top = jnp.max(masked, axis=-1)
    expo = jnp.where(live[None, None, None, :], jnp.exp(masked - top[..., None]), 0.0)
    totals = jnp.sum(expo, axis=-1)
    mixed = jnp.einsum(
        "shqk,skhd->sqhd", expo.astype(jnp.bfloat16), v, preferred_element_type=jnp.float32
    )
    context = (mixed / jnp.transpose(totals, (0, 2, 1))[..., None]).astype(jnp.bfloat16)
    context = context.reshape(spec_mine, q_slots, heads_here * HD)
    context = jnp.swapaxes(context.reshape(spec_mine, n_z, -1), 0, 1).reshape(n_z, -1)
    context_rows = lax.all_to_all(context, "z", 0, 0, tiled=True)
    context_rows = context_rows.reshape(spec, slots_here, heads_here * HD)
    n_band = lax.axis_size("band")
    context_rows = context_rows.reshape(n_band, spec_here, slots_here, heads_here * HD)
    context_rows = jnp.swapaxes(context_rows, 1, 2).reshape(spec * slots_here, heads_here * HD)
    out = jnp.dot(context_rows, w_out, preferred_element_type=jnp.float32).astype(jnp.bfloat16)
    attn_out = band_sum(out.reshape(n_band, slots_here, spec_here, width))
    state = (kept_rows.astype(jnp.float32) + attn_out).astype(jnp.bfloat16)
    mlp_in = band_gather(normed(state, mlp_gain))
    piece = jnp.swapaxes(mlp_in.reshape(n_band, spec_here, slots_here, width), 1, 2)
    piece = piece.reshape(spec * slots_here, width)
    gate = jnp.dot(piece, w_gate, preferred_element_type=jnp.float32)
    upper = jnp.dot(piece, w_up, preferred_element_type=jnp.float32)
    hidden = (jax.nn.silu(gate) * upper).astype(jnp.bfloat16)
    out = jnp.dot(hidden, w_down, preferred_element_type=jnp.float32).astype(jnp.bfloat16)
    mlp_out = band_sum(out.reshape(n_band, slots_here, spec_here, width))
    encoded = (state.astype(jnp.float32) + mlp_out).astype(jnp.bfloat16)
    chosen = (
        jnp.arange(pixels.shape[0], dtype=jnp.int32)[:, None] == clear_index[None, :]
    ) & live_here[None, :]
    placed = jnp.einsum(
        "pc,scd->psd", chosen.astype(jnp.bfloat16), encoded, preferred_element_type=jnp.float32
    ).astype(jnp.bfloat16)
    taken = jnp.any(chosen, axis=1)
    return jnp.where(taken[:, None, None], placed, pixels)


def solution(mesh):
    n_band, n_pix = mesh.devices.shape
    split = Mesh(mesh.devices.reshape(n_band, n_pix // 2, 2), ("band", "z", "c"))
    pix = ("z", "c")
    return jax.shard_map(
        shards,
        mesh=split,
        in_specs=(
            P(pix, "band", None),
            P(pix),
            P(pix),
            P(),
            P(None, "band"),
            P(None, "band"),
            P(None, "band"),
            P("band", None),
            P(),
            P(None, "band"),
            P(None, "band"),
            P("band", None),
        ),
        out_specs=P(pix, "band", None),
        check_vma=False,
    )
```

```python
import jax
import jax.numpy as jnp
from jax import lax
from jax.sharding import Mesh, PartitionSpec as P

HD = 64


def normed(rows, gain):
    full = rows.astype(jnp.float32)
    scaled = full * lax.rsqrt(jnp.mean(full * full, axis=-1, keepdims=True) + 1e-05)
    return (scaled * gain).astype(jnp.bfloat16)


def band_gather(rows):
    n = lax.axis_size("band")
    sent = jnp.broadcast_to(rows[None], (n,) + rows.shape)
    got = lax.all_to_all(sent, "band", 0, 0, tiled=True)
    return got.reshape((n * rows.shape[0],) + rows.shape[1:])


def band_reduce(part):
    n = lax.axis_size("band")
    split = part.reshape((n, part.shape[0] // n) + part.shape[1:])
    got = lax.all_to_all(split, "band", 0, 0, tiled=True)
    return jnp.sum(got.astype(jnp.float32), axis=0)


def band_sum(part):
    got = lax.all_to_all(jnp.swapaxes(part, 1, 2), "band", 0, 0, tiled=True)
    return jnp.sum(got.astype(jnp.float32), axis=0)


def shards(
    pixels,
    clear_count,
    clear_index,
    attn_gain,
    w_query,
    w_key,
    w_value,
    w_out,
    mlp_gain,
    w_gate,
    w_up,
    w_down,
):
    own_count = clear_count[0]
    kept = jnp.take(pixels, clear_index, axis=0)
    kept_rows = jnp.swapaxes(kept, 0, 1)
    spec_here, slots_here, width = kept_rows.shape
    attn_in = band_gather(normed(kept_rows, attn_gain))
    spec = attn_in.shape[0]
    flat = attn_in.reshape(spec * slots_here, width)
    heads_here = w_query.shape[1] // HD

    def project(weight):
        out = jnp.dot(flat, weight, preferred_element_type=jnp.float32).astype(jnp.bfloat16)
        return out.reshape(spec, slots_here, heads_here * HD)

    live_here = jnp.arange(slots_here, dtype=jnp.int32) < own_count
    qkv = jnp.concatenate([project(w_query), project(w_key), project(w_value)], axis=-1)
    width_qkv = qkv.shape[-1]
    flag_row = jnp.zeros((spec, 1, width_qkv), jnp.bfloat16)
    at = heads_here * HD
    flag_row = flag_row.at[:, 0, at : at + slots_here].set(live_here.astype(jnp.bfloat16)[None, :])
    payload = jnp.concatenate([qkv, flag_row], axis=1)
    n_z = lax.axis_size("z")
    spec_mine = spec // n_z
    mine = lax.all_to_all(payload.reshape(n_z, spec_mine, -1), "z", 0, 0, tiled=True)
    mine = mine.reshape(n_z, spec_mine, slots_here + 1, width_qkv)
    mine = jnp.swapaxes(mine, 0, 1)
    kv_flag = mine[..., heads_here * HD :]
    other = lax.ppermute(kv_flag, "c", [(0, 1), (1, 0)])
    kv_flag = jnp.concatenate([kv_flag, other], axis=1)
    live = (kv_flag[0, :, slots_here, :slots_here] > 0.5).reshape(-1)
    kv = kv_flag[:, :, :slots_here].reshape(spec_mine, -1, 2 * heads_here * HD)
    q_slots = n_z * slots_here
    q = mine[:, :, :slots_here, : heads_here * HD].reshape(spec_mine, q_slots, heads_here, HD)
    k = kv[..., : heads_here * HD].reshape(spec_mine, -1, heads_here, HD)
    v = kv[..., heads_here * HD :].reshape(spec_mine, -1, heads_here, HD)
    scores = jnp.einsum("sqhd,skhd->shqk", q, k, preferred_element_type=jnp.float32) * HD ** (-0.5)
    masked = jnp.where(live[None, None, None, :], scores, -1e30)
    top = jnp.max(masked, axis=-1)
    expo = jnp.where(live[None, None, None, :], jnp.exp(masked - top[..., None]), 0.0)
    totals = jnp.sum(expo, axis=-1)
    mixed = jnp.einsum(
        "shqk,skhd->sqhd", expo.astype(jnp.bfloat16), v, preferred_element_type=jnp.float32
    )
    context = (mixed / jnp.transpose(totals, (0, 2, 1))[..., None]).astype(jnp.bfloat16)
    context = context.reshape(spec_mine, q_slots, heads_here * HD)
    context = jnp.swapaxes(context.reshape(spec_mine, n_z, -1), 0, 1)
    context_rows = lax.all_to_all(context, "z", 0, 0, tiled=True)
    context_rows = context_rows.reshape(spec, slots_here, heads_here * HD)
    n_band = lax.axis_size("band")
    context_rows = context_rows.reshape(n_band, spec_here, slots_here, heads_here * HD)
    context_rows = jnp.swapaxes(context_rows, 1, 2).reshape(spec * slots_here, heads_here * HD)
    out = jnp.dot(context_rows, w_out, preferred_element_type=jnp.float32).astype(jnp.bfloat16)
    attn_out = band_sum(out.reshape(n_band, slots_here, spec_here, width))
    state = (kept_rows.astype(jnp.float32) + attn_out).astype(jnp.bfloat16)
    mlp_in = band_gather(normed(state, mlp_gain))
    piece = jnp.swapaxes(mlp_in.reshape(n_band, spec_here, slots_here, width), 1, 2)
    piece = piece.reshape(spec * slots_here, width)
    gate = jnp.dot(piece, w_gate, preferred_element_type=jnp.float32)
    upper = jnp.dot(piece, w_up, preferred_element_type=jnp.float32)
    hidden = (jax.nn.silu(gate) * upper).astype(jnp.bfloat16)
    out = jnp.dot(hidden, w_down, preferred_element_type=jnp.float32).astype(jnp.bfloat16)
    mlp_out = band_sum(out.reshape(n_band, slots_here, spec_here, width))
    encoded = (state.astype(jnp.float32) + mlp_out).astype(jnp.bfloat16)
    chosen = (
        jnp.arange(pixels.shape[0], dtype=jnp.int32)[:, None] == clear_index[None, :]
    ) & live_here[None, :]
    placed = jnp.einsum(
        "pc,scd->psd", chosen.astype(jnp.bfloat16), encoded, preferred_element_type=jnp.float32
    ).astype(jnp.bfloat16)
    taken = jnp.any(chosen, axis=1)
    return jnp.where(taken[:, None, None], placed, pixels)


def solution(mesh):
    n_band, n_pix = mesh.devices.shape
    split = Mesh(mesh.devices.reshape(n_band, n_pix // 2, 2), ("band", "z", "c"))
    pix = ("z", "c")
    return jax.shard_map(
        shards,
        mesh=split,
        in_specs=(
            P(pix, "band", None),
            P(pix),
            P(pix),
            P(),
            P(None, "band"),
            P(None, "band"),
            P(None, "band"),
            P("band", None),
            P(),
            P(None, "band"),
            P(None, "band"),
            P("band", None),
        ),
        out_specs=P(pix, "band", None),
        check_vma=False,
    )
```

```python
import jax
import jax.numpy as jnp
from jax import lax
from jax.sharding import Mesh, PartitionSpec as P

HD = 64


def normed(rows, gain):
    full = rows.astype(jnp.float32)
    scaled = full * lax.rsqrt(jnp.mean(full * full, axis=-1, keepdims=True) + 1e-05)
    return (scaled * gain).astype(jnp.bfloat16)


def band_gather(rows):
    n = lax.axis_size("band")
    sent = jnp.broadcast_to(rows[None], (n,) + rows.shape)
    return lax.all_to_all(sent, "band", 0, 0, tiled=True)


def band_sum(part):
    got = lax.all_to_all(part, "band", 0, 0, tiled=True)
    return jnp.sum(got.astype(jnp.float32), axis=0)


def shards(
    pixels,
    clear_count,
    clear_index,
    attn_gain,
    w_query,
    w_key,
    w_value,
    w_out,
    mlp_gain,
    w_gate,
    w_up,
    w_down,
):
    own_count = clear_count[0]
    kept = jnp.take(pixels, clear_index, axis=0)
    slots_here, spec_here, width = kept.shape
    n_band = lax.axis_size("band")
    spec = n_band * spec_here
    attn_in = band_gather(normed(kept, attn_gain))
    flat = attn_in.reshape(-1, width)
    heads_here = w_query.shape[1] // HD

    def project(weight):
        out = jnp.dot(flat, weight, preferred_element_type=jnp.float32).astype(jnp.bfloat16)
        return out.reshape(n_band, slots_here, spec_here, heads_here * HD)

    live_here = jnp.arange(slots_here, dtype=jnp.int32) < own_count
    qkv = jnp.concatenate([project(w_query), project(w_key), project(w_value)], axis=-1)
    qkv = jnp.swapaxes(qkv, 1, 2)
    width_qkv = qkv.shape[-1]
    at = heads_here * HD
    flags = jnp.zeros((width_qkv,), jnp.bfloat16).at[at : at + slots_here].set(live_here.astype(jnp.bfloat16))
    flag_row = jnp.broadcast_to(flags, (n_band, spec_here, 1, width_qkv))
    payload = jnp.concatenate([qkv, flag_row], axis=2)
    n_z = lax.axis_size("z")
    spec_mine = spec // n_z
    mine = lax.all_to_all(payload.reshape(n_z, spec_mine, -1), "z", 0, 0, tiled=True)
    mine = mine.reshape(n_z, spec_mine, slots_here + 1, width_qkv)
    mine = jnp.swapaxes(mine, 0, 1)
    kv_flag = mine[..., heads_here * HD :]
    other = lax.ppermute(kv_flag, "c", [(0, 1), (1, 0)])
    kv_flag = jnp.concatenate([kv_flag, other], axis=1)
    live = (kv_flag[0, :, slots_here, :slots_here] > 0.5).reshape(-1)
    kv = kv_flag[:, :, :slots_here].reshape(spec_mine, -1, 2 * heads_here * HD)
    q_slots = n_z * slots_here
    q = mine[:, :, :slots_here, : heads_here * HD].reshape(spec_mine, q_slots, heads_here, HD)
    k = kv[..., : heads_here * HD].reshape(spec_mine, -1, heads_here, HD)
    v = kv[..., heads_here * HD :].reshape(spec_mine, -1, heads_here, HD)
    scores = jnp.einsum("sqhd,skhd->shqk", q, k, preferred_element_type=jnp.float32) * HD ** (-0.5)
    masked = jnp.where(live[None, None, None, :], scores, -1e30)
    top = jnp.max(masked, axis=-1)
    expo = jnp.where(live[None, None, None, :], jnp.exp(masked - top[..., None]), 0.0)
    totals = jnp.sum(expo, axis=-1)
    mixed = jnp.einsum(
        "shqk,skhd->sqhd", expo.astype(jnp.bfloat16), v, preferred_element_type=jnp.float32
    )
    context = (mixed / jnp.transpose(totals, (0, 2, 1))[..., None]).astype(jnp.bfloat16)
    context = context.reshape(spec_mine, q_slots, heads_here * HD)
    context = jnp.swapaxes(context.reshape(spec_mine, n_z, -1), 0, 1)
    context_rows = lax.all_to_all(context, "z", 0, 0, tiled=True)
    context_rows = context_rows.reshape(n_band, spec_here, slots_here, heads_here * HD)
    context_rows = jnp.swapaxes(context_rows, 1, 2).reshape(-1, heads_here * HD)
    out = jnp.dot(context_rows, w_out, preferred_element_type=jnp.float32).astype(jnp.bfloat16)
    attn_out = band_sum(out.reshape(n_band, slots_here, spec_here, width))
    state = (kept.astype(jnp.float32) + attn_out).astype(jnp.bfloat16)
    mlp_in = band_gather(normed(state, mlp_gain))
    piece = mlp_in.reshape(-1, width)
    gate = jnp.dot(piece, w_gate, preferred_element_type=jnp.float32)
    upper = jnp.dot(piece, w_up, preferred_element_type=jnp.float32)
    hidden = (jax.nn.silu(gate) * upper).astype(jnp.bfloat16)
    out = jnp.dot(hidden, w_down, preferred_element_type=jnp.float32).astype(jnp.bfloat16)
    mlp_out = band_sum(out.reshape(n_band, slots_here, spec_here, width))
    encoded = (state.astype(jnp.float32) + mlp_out).astype(jnp.bfloat16)
    chosen = (
        jnp.arange(pixels.shape[0], dtype=jnp.int32)[:, None] == clear_index[None, :]
    ) & live_here[None, :]
    placed = jnp.einsum(
        "pc,csd->psd", chosen.astype(jnp.bfloat16), encoded, preferred_element_type=jnp.float32
    ).astype(jnp.bfloat16)
    taken = jnp.any(chosen, axis=1)
    return jnp.where(taken[:, None, None], placed, pixels)


def solution(mesh):
    n_band, n_pix = mesh.devices.shape
    split = Mesh(mesh.devices.reshape(n_band, n_pix // 2, 2), ("band", "z", "c"))
    pix = ("z", "c")
    return jax.shard_map(
        shards,
        mesh=split,
        in_specs=(
            P(pix, "band", None),
            P(pix),
            P(pix),
            P(),
            P(None, "band"),
            P(None, "band"),
            P(None, "band"),
            P("band", None),
            P(),
            P(None, "band"),
            P(None, "band"),
            P("band", None),
        ),
        out_specs=P(pix, "band", None),
        check_vma=False,
    )
```

```python
import jax
import jax.numpy as jnp
from jax import lax
from jax.sharding import Mesh, PartitionSpec as P

HD = 64


def normed(rows, gain):
    full = rows.astype(jnp.float32)
    scaled = full * lax.rsqrt(jnp.mean(full * full, axis=-1, keepdims=True) + 1e-05)
    return (scaled * gain).astype(jnp.bfloat16)


def band_gather(rows):
    n = lax.axis_size("band")
    sent = jnp.broadcast_to(rows[None], (n,) + rows.shape)
    return lax.all_to_all(sent, "band", 0, 0, tiled=True)


def band_sum(part):
    got = lax.all_to_all(part, "band", 0, 0, tiled=True)
    return jnp.sum(got.astype(jnp.float32), axis=0)


def shards(
    pixels,
    clear_count,
    clear_index,
    attn_gain,
    w_query,
    w_key,
    w_value,
    w_out,
    mlp_gain,
    w_gate,
    w_up,
    w_down,
):
    own_count = clear_count[0]
    kept = jnp.take(pixels, clear_index, axis=0, mode="clip")
    slots_here, spec_here, width = kept.shape
    n_band = lax.axis_size("band")
    spec = n_band * spec_here
    attn_in = band_gather(jnp.take(normed(pixels, attn_gain), clear_index, axis=0, mode="clip"))
    flat = attn_in.reshape(-1, width)
    heads_here = w_query.shape[1] // HD

    def project(weight):
        out = jnp.dot(flat, weight, preferred_element_type=jnp.float32).astype(jnp.bfloat16)
        return out.reshape(n_band, slots_here, spec_here, heads_here * HD)

    live_here = jnp.arange(slots_here, dtype=jnp.int32) < own_count
    qkv = jnp.concatenate([project(w_query), project(w_key), project(w_value)], axis=-1)
    qkv = jnp.swapaxes(qkv, 1, 2)
    width_qkv = qkv.shape[-1]
    at = heads_here * HD
    flags = jnp.zeros((width_qkv,), jnp.bfloat16).at[at : at + slots_here].set(live_here.astype(jnp.bfloat16))
    flag_row = jnp.broadcast_to(flags, (n_band, spec_here, 1, width_qkv))
    payload = jnp.concatenate([qkv, flag_row], axis=2)
    n_z = lax.axis_size("z")
    spec_mine = spec // n_z
    mine = lax.all_to_all(payload.reshape(n_z, spec_mine, -1), "z", 0, 0, tiled=True)
    mine = mine.reshape(n_z, spec_mine, slots_here + 1, width_qkv)
    mine = jnp.swapaxes(mine, 0, 1)
    kv_flag = mine[..., heads_here * HD :]
    other = lax.ppermute(kv_flag, "c", [(0, 1), (1, 0)])
    kv_flag = jnp.concatenate([kv_flag, other], axis=1)
    live = (kv_flag[0, :, slots_here, :slots_here] > 0.5).reshape(-1)
    kv = kv_flag[:, :, :slots_here].reshape(spec_mine, -1, 2 * heads_here * HD)
    q_slots = n_z * slots_here
    q = mine[:, :, :slots_here, : heads_here * HD].reshape(spec_mine, q_slots, heads_here, HD)
    k = kv[..., : heads_here * HD].reshape(spec_mine, -1, heads_here, HD)
    v = kv[..., heads_here * HD :].reshape(spec_mine, -1, heads_here, HD)
    scores = jnp.einsum("sqhd,skhd->shqk", q, k, preferred_element_type=jnp.float32) * HD ** (-0.5)
    masked = jnp.where(live[None, None, None, :], scores, -1e30)
    top = jnp.max(masked, axis=-1)
    expo = jnp.where(live[None, None, None, :], jnp.exp(masked - top[..., None]), 0.0)
    totals = jnp.sum(expo, axis=-1)
    mixed = jnp.einsum(
        "shqk,skhd->sqhd", expo.astype(jnp.bfloat16), v, preferred_element_type=jnp.float32
    )
    context = (mixed / jnp.transpose(totals, (0, 2, 1))[..., None]).astype(jnp.bfloat16)
    context = context.reshape(spec_mine, q_slots, heads_here * HD)
    context = jnp.swapaxes(context.reshape(spec_mine, n_z, -1), 0, 1)
    context_rows = lax.all_to_all(context, "z", 0, 0, tiled=True)
    context_rows = context_rows.reshape(n_band, spec_here, slots_here, heads_here * HD)
    context_rows = jnp.swapaxes(context_rows, 1, 2).reshape(-1, heads_here * HD)
    out = jnp.dot(context_rows, w_out, preferred_element_type=jnp.float32).astype(jnp.bfloat16)
    attn_out = band_sum(out.reshape(n_band, slots_here, spec_here, width))
    state = (kept.astype(jnp.float32) + attn_out).astype(jnp.bfloat16)
    mlp_in = band_gather(normed(state, mlp_gain))
    piece = mlp_in.reshape(-1, width)
    gate = jnp.dot(piece, w_gate, preferred_element_type=jnp.float32)
    upper = jnp.dot(piece, w_up, preferred_element_type=jnp.float32)
    hidden = (jax.nn.silu(gate) * upper).astype(jnp.bfloat16)
    out = jnp.dot(hidden, w_down, preferred_element_type=jnp.float32).astype(jnp.bfloat16)
    mlp_out = band_sum(out.reshape(n_band, slots_here, spec_here, width))
    encoded = (state.astype(jnp.float32) + mlp_out).astype(jnp.bfloat16)
    chosen = (
        jnp.arange(pixels.shape[0], dtype=jnp.int32)[:, None] == clear_index[None, :]
    ) & live_here[None, :]
    placed = jnp.einsum(
        "pc,csd->psd", chosen.astype(jnp.bfloat16), encoded, preferred_element_type=jnp.float32
    ).astype(jnp.bfloat16)
    taken = jnp.any(chosen, axis=1)
    return jnp.where(taken[:, None, None], placed, pixels)


def solution(mesh):
    n_band, n_pix = mesh.devices.shape
    split = Mesh(mesh.devices.reshape(n_band, n_pix // 2, 2), ("band", "z", "c"))
    pix = ("z", "c")
    return jax.shard_map(
        shards,
        mesh=split,
        in_specs=(
            P(pix, "band", None),
            P(pix),
            P(pix),
            P(),
            P(None, "band"),
            P(None, "band"),
            P(None, "band"),
            P("band", None),
            P(),
            P(None, "band"),
            P(None, "band"),
            P("band", None),
        ),
        out_specs=P(pix, "band", None),
        check_vma=False,
    )
```

```python
import jax
import jax.numpy as jnp
from jax import lax
from jax.sharding import Mesh, PartitionSpec as P

HD = 64


def normed(rows, gain):
    full = rows.astype(jnp.float32)
    scaled = full * lax.rsqrt(jnp.mean(full * full, axis=-1, keepdims=True) + 1e-05)
    return (scaled * gain).astype(jnp.bfloat16)


def band_gather(rows):
    n = lax.axis_size("band")
    sent = jnp.broadcast_to(rows[None], (n,) + rows.shape)
    return lax.all_to_all(sent, "band", 0, 0, tiled=True)


def band_sum(part):
    got = lax.all_to_all(part, "band", 0, 0, tiled=True)
    return jnp.sum(got.astype(jnp.float32), axis=0)


def shards(
    pixels,
    clear_count,
    clear_index,
    attn_gain,
    w_query,
    w_key,
    w_value,
    w_out,
    mlp_gain,
    w_gate,
    w_up,
    w_down,
):
    own_count = clear_count[0]
    kept = jnp.take(pixels, clear_index, axis=0, mode="clip")
    slots_here, spec_here, width = kept.shape
    n_band = lax.axis_size("band")
    spec = n_band * spec_here
    attn_in = band_gather(jnp.take(normed(pixels, attn_gain), clear_index, axis=0, mode="clip"))
    flat = attn_in.reshape(-1, width)
    heads_here = w_query.shape[1] // HD

    live_here = jnp.arange(slots_here, dtype=jnp.int32) < own_count
    w_qkv = jnp.concatenate([w_query, w_key, w_value], axis=1)
    qkv = jnp.dot(flat, w_qkv, preferred_element_type=jnp.float32).astype(jnp.bfloat16)
    qkv = jnp.swapaxes(qkv.reshape(n_band, slots_here, spec_here, -1), 1, 2)
    width_qkv = qkv.shape[-1]
    n_flag = 64
    flags = jnp.pad(live_here.astype(jnp.bfloat16), (0, n_flag - slots_here))
    flags = jnp.broadcast_to(flags, (n_band, spec_here, n_flag))
    payload = jnp.concatenate([qkv.reshape(n_band, spec_here, -1), flags], axis=2)
    n_z = lax.axis_size("z")
    spec_mine = spec // n_z
    mine = lax.all_to_all(payload.reshape(n_z, spec_mine, -1), "z", 0, 0, tiled=True)
    live_mine = mine[:, 0, slots_here * width_qkv :]
    mine = mine[..., : slots_here * width_qkv].reshape(n_z, spec_mine, slots_here, width_qkv)
    mine = jnp.swapaxes(mine, 0, 1)
    kv = mine[..., heads_here * HD :]
    flag_rows = jnp.pad(live_mine, ((0, 0), (0, kv.shape[-1] - n_flag)))
    kv_flag = jnp.concatenate([kv, jnp.broadcast_to(flag_rows[None, :, None], (spec_mine,) + flag_rows.shape[:1] + (1, kv.shape[-1]))], axis=2)
    other = lax.ppermute(kv_flag, "c", [(0, 1), (1, 0)])
    kv_flag = jnp.concatenate([kv_flag, other], axis=1)
    live = (kv_flag[0, :, slots_here, :slots_here] > 0.5).reshape(-1)
    kv = kv_flag[:, :, :slots_here].reshape(spec_mine, -1, 2 * heads_here * HD)
    q_slots = n_z * slots_here
    q = mine[:, :, :slots_here, : heads_here * HD].reshape(spec_mine, q_slots, heads_here, HD)
    k = kv[..., : heads_here * HD].reshape(spec_mine, -1, heads_here, HD)
    v = kv[..., heads_here * HD :].reshape(spec_mine, -1, heads_here, HD)
    scores = jnp.einsum("sqhd,skhd->shqk", q, k, preferred_element_type=jnp.float32) * HD ** (-0.5)
    masked = jnp.where(live[None, None, None, :], scores, -1e30)
    top = jnp.max(masked, axis=-1)
    expo = jnp.where(live[None, None, None, :], jnp.exp(masked - top[..., None]), 0.0)
    totals = jnp.sum(expo, axis=-1)
    mixed = jnp.einsum(
        "shqk,skhd->sqhd", expo.astype(jnp.bfloat16), v, preferred_element_type=jnp.float32
    )
    context = (mixed / jnp.transpose(totals, (0, 2, 1))[..., None]).astype(jnp.bfloat16)
    context = context.reshape(spec_mine, q_slots, heads_here * HD)
    context = jnp.swapaxes(context.reshape(spec_mine, n_z, -1), 0, 1)
    context_rows = lax.all_to_all(context, "z", 0, 0, tiled=True)
    context_rows = context_rows.reshape(n_band, spec_here, slots_here, heads_here * HD)
    context_rows = jnp.swapaxes(context_rows, 1, 2)
    out = jnp.einsum("bsjh,hd->bsjd", context_rows, w_out, preferred_element_type=jnp.float32)
    attn_out = band_sum(out.astype(jnp.bfloat16))
    state = (kept.astype(jnp.float32) + attn_out).astype(jnp.bfloat16)
    mlp_in = band_gather(normed(state, mlp_gain))
    gate = jnp.einsum("bsjd,df->bsjf", mlp_in, w_gate, preferred_element_type=jnp.float32)
    upper = jnp.einsum("bsjd,df->bsjf", mlp_in, w_up, preferred_element_type=jnp.float32)
    hidden = (jax.nn.silu(gate) * upper).astype(jnp.bfloat16)
    out = jnp.einsum("bsjf,fd->bsjd", hidden, w_down, preferred_element_type=jnp.float32)
    mlp_out = band_sum(out.astype(jnp.bfloat16))
    encoded = (state.astype(jnp.float32) + mlp_out).astype(jnp.bfloat16)
    chosen = (
        jnp.arange(pixels.shape[0], dtype=jnp.int32)[:, None] == clear_index[None, :]
    ) & live_here[None, :]
    placed = jnp.einsum(
        "pc,csd->psd", chosen.astype(jnp.bfloat16), encoded, preferred_element_type=jnp.float32
    ).astype(jnp.bfloat16)
    taken = jnp.any(chosen, axis=1)
    return jnp.where(taken[:, None, None], placed, pixels)


def solution(mesh):
    n_band, n_pix = mesh.devices.shape
    split = Mesh(mesh.devices.reshape(n_band, n_pix // 2, 2), ("band", "z", "c"))
    pix = ("z", "c")
    return jax.shard_map(
        shards,
        mesh=split,
        in_specs=(
            P(pix, "band", None),
            P(pix),
            P(pix),
            P(),
            P(None, "band"),
            P(None, "band"),
            P(None, "band"),
            P("band", None),
            P(),
            P(None, "band"),
            P(None, "band"),
            P("band", None),
        ),
        out_specs=P(pix, "band", None),
        check_vma=False,
    )
```

```python
import jax
import jax.numpy as jnp
from jax import lax
from jax.sharding import Mesh, PartitionSpec as P

HD = 64


def normed(rows, gain):
    full = rows.astype(jnp.float32)
    scaled = full * lax.rsqrt(jnp.mean(full * full, axis=-1, keepdims=True) + 1e-05)
    return (scaled * gain).astype(jnp.bfloat16)


def band_gather(rows):
    n = lax.axis_size("band")
    sent = jnp.broadcast_to(rows[None], (n,) + rows.shape)
    return lax.all_to_all(sent, "band", 0, 0, tiled=True)


def band_sum(part):
    got = lax.all_to_all(part, "band", 0, 0, tiled=True)
    return jnp.sum(got.astype(jnp.float32), axis=0)


def shards(
    pixels,
    clear_count,
    clear_index,
    attn_gain,
    w_query,
    w_key,
    w_value,
    w_out,
    mlp_gain,
    w_gate,
    w_up,
    w_down,
):
    own_count = clear_count[0]
    kept = jnp.take(pixels, clear_index, axis=0, mode="clip")
    slots_here, spec_here, width = kept.shape
    n_band = lax.axis_size("band")
    spec = n_band * spec_here
    attn_in = band_gather(jnp.take(normed(pixels, attn_gain), clear_index, axis=0, mode="clip"))
    flat = attn_in.reshape(-1, width)
    heads_here = w_query.shape[1] // HD

    live_here = jnp.arange(slots_here, dtype=jnp.int32) < own_count
    w_qkv = jnp.concatenate([w_query, w_key, w_value], axis=1)
    qkv = jnp.dot(flat, w_qkv, preferred_element_type=jnp.float32).astype(jnp.bfloat16)
    qkv = jnp.swapaxes(qkv.reshape(n_band, slots_here, spec_here, -1), 1, 2)
    width_qkv = qkv.shape[-1]
    n_flag = 64
    flags = jnp.pad(live_here.astype(jnp.bfloat16), (0, n_flag - slots_here))
    flags = jnp.broadcast_to(flags, (n_band, spec_here, n_flag))
    payload = jnp.concatenate([qkv.reshape(n_band, spec_here, -1), flags], axis=2)
    pix = ("z", "c")
    n_pix = lax.axis_size(pix)
    mine = lax.all_to_all(payload.reshape(n_pix, spec // n_pix, -1), pix, 0, 0, tiled=True)
    live = (mine[:, 0, slots_here * width_qkv : slots_here * width_qkv + slots_here] > 0.5).reshape(-1)
    rows = mine[..., : slots_here * width_qkv].reshape(-1, n_pix * slots_here, width_qkv)
    spec_mine = rows.shape[0]
    q = rows[..., : heads_here * HD].reshape(spec_mine, -1, heads_here, HD)
    k = rows[..., heads_here * HD : 2 * heads_here * HD].reshape(spec_mine, -1, heads_here, HD)
    v = rows[..., 2 * heads_here * HD :].reshape(spec_mine, -1, heads_here, HD)
    scores = jnp.einsum("sqhd,skhd->shqk", q, k, preferred_element_type=jnp.float32) * HD ** (-0.5)
    masked = jnp.where(live[None, None, None, :], scores, -1e30)
    top = jnp.max(masked, axis=-1)
    expo = jnp.where(live[None, None, None, :], jnp.exp(masked - top[..., None]), 0.0)
    totals = jnp.sum(expo, axis=-1)
    mixed = jnp.einsum(
        "shqk,skhd->sqhd", expo.astype(jnp.bfloat16), v, preferred_element_type=jnp.float32
    )
    context = (mixed / jnp.transpose(totals, (0, 2, 1))[..., None]).astype(jnp.bfloat16)
    context = jnp.swapaxes(context.reshape(spec_mine, n_pix, -1), 0, 1)
    context_rows = lax.all_to_all(context, pix, 0, 0, tiled=True)
    context_rows = context_rows.reshape(n_band, spec_here, slots_here, heads_here * HD)
    context_rows = jnp.swapaxes(context_rows, 1, 2)
    out = jnp.einsum("bsjh,hd->bsjd", context_rows, w_out, preferred_element_type=jnp.float32)
    attn_out = band_sum(out.astype(jnp.bfloat16))
    state = (kept.astype(jnp.float32) + attn_out).astype(jnp.bfloat16)
    mlp_in = band_gather(normed(state, mlp_gain))
    gate = jnp.einsum("bsjd,df->bsjf", mlp_in, w_gate, preferred_element_type=jnp.float32)
    upper = jnp.einsum("bsjd,df->bsjf", mlp_in, w_up, preferred_element_type=jnp.float32)
    hidden = (jax.nn.silu(gate) * upper).astype(jnp.bfloat16)
    out = jnp.einsum("bsjf,fd->bsjd", hidden, w_down, preferred_element_type=jnp.float32)
    mlp_out = band_sum(out.astype(jnp.bfloat16))
    encoded = (state.astype(jnp.float32) + mlp_out).astype(jnp.bfloat16)
    chosen = (
        jnp.arange(pixels.shape[0], dtype=jnp.int32)[:, None] == clear_index[None, :]
    ) & live_here[None, :]
    placed = jnp.einsum(
        "pc,csd->psd", chosen.astype(jnp.bfloat16), encoded, preferred_element_type=jnp.float32
    ).astype(jnp.bfloat16)
    taken = jnp.any(chosen, axis=1)
    return jnp.where(taken[:, None, None], placed, pixels)


def solution(mesh):
    n_band, n_pix = mesh.devices.shape
    split = Mesh(mesh.devices.reshape(n_band, n_pix // 2, 2), ("band", "z", "c"))
    pix = ("z", "c")
    return jax.shard_map(
        shards,
        mesh=split,
        in_specs=(
            P(pix, "band", None),
            P(pix),
            P(pix),
            P(),
            P(None, "band"),
            P(None, "band"),
            P(None, "band"),
            P("band", None),
            P(),
            P(None, "band"),
            P(None, "band"),
            P("band", None),
        ),
        out_specs=P(pix, "band", None),
        check_vma=False,
    )
```

```python
import jax
import jax.numpy as jnp
from jax import lax
from jax.sharding import Mesh, PartitionSpec as P

HD = 64


def normed(rows, gain):
    full = rows.astype(jnp.float32)
    scaled = full * lax.rsqrt(jnp.mean(full * full, axis=-1, keepdims=True) + 1e-05)
    return (scaled * gain).astype(jnp.bfloat16)


def band_gather(rows):
    n = lax.axis_size("band")
    sent = jnp.broadcast_to(rows[None], (n,) + rows.shape)
    return lax.all_to_all(sent, "band", 0, 0, tiled=True)


def band_sum(part):
    got = lax.all_to_all(part, "band", 0, 0, tiled=True)
    return jnp.sum(got.astype(jnp.float32), axis=0)


def shards(
    pixels,
    clear_count,
    clear_index,
    attn_gain,
    w_query,
    w_key,
    w_value,
    w_out,
    mlp_gain,
    w_gate,
    w_up,
    w_down,
):
    own_count = clear_count[0]
    kept = jnp.take(pixels, clear_index, axis=0, mode="clip")
    slots_here, spec_here, width = kept.shape
    n_band = lax.axis_size("band")
    spec = n_band * spec_here
    attn_in = band_gather(jnp.take(normed(pixels, attn_gain), clear_index, axis=0, mode="clip"))
    flat = attn_in.reshape(-1, width)
    heads_here = w_query.shape[1] // HD

    live_here = jnp.arange(slots_here, dtype=jnp.int32) < own_count
    w_qkv = jnp.concatenate([w_query, w_key, w_value], axis=1)
    qkv = jnp.dot(flat, w_qkv, preferred_element_type=jnp.bfloat16)
    qkv = jnp.swapaxes(qkv.reshape(n_band, slots_here, spec_here, -1), 1, 2)
    width_qkv = qkv.shape[-1]
    n_flag = 64
    flags = jnp.pad(live_here.astype(jnp.bfloat16), (0, n_flag - slots_here))
    flags = jnp.broadcast_to(flags, (n_band, spec_here, n_flag))
    payload = jnp.concatenate([qkv.reshape(n_band, spec_here, -1), flags], axis=2)
    n_z = lax.axis_size("z")
    spec_mine = spec // n_z
    mine = lax.all_to_all(payload.reshape(n_z, spec_mine, -1), "z", 0, 0, tiled=True)
    live_mine = mine[:, 0, slots_here * width_qkv :]
    mine = mine[..., : slots_here * width_qkv].reshape(n_z, spec_mine, slots_here, width_qkv)
    mine = jnp.swapaxes(mine, 0, 1)
    kv = mine[..., heads_here * HD :]
    flag_rows = jnp.pad(live_mine, ((0, 0), (0, kv.shape[-1] - n_flag)))
    kv_flag = jnp.concatenate([kv, jnp.broadcast_to(flag_rows[None, :, None], (spec_mine,) + flag_rows.shape[:1] + (1, kv.shape[-1]))], axis=2)
    other = lax.ppermute(kv_flag, "c", [(0, 1), (1, 0)])
    kv_flag = jnp.concatenate([kv_flag, other], axis=1)
    live = (kv_flag[0, :, slots_here, :slots_here] > 0.5).reshape(-1)
    kv = kv_flag[:, :, :slots_here].reshape(spec_mine, -1, 2 * heads_here * HD)
    q_slots = n_z * slots_here
    q = mine[:, :, :slots_here, : heads_here * HD].reshape(spec_mine, q_slots, heads_here, HD)
    k = kv[..., : heads_here * HD].reshape(spec_mine, -1, heads_here, HD)
    v = kv[..., heads_here * HD :].reshape(spec_mine, -1, heads_here, HD)
    scores = jnp.einsum("sqhd,skhd->shqk", q, k, preferred_element_type=jnp.float32) * HD ** (-0.5)
    masked = jnp.where(live[None, None, None, :], scores, -1e30)
    top = jnp.max(masked, axis=-1)
    expo = jnp.where(live[None, None, None, :], jnp.exp(masked - top[..., None]), 0.0)
    totals = jnp.sum(expo, axis=-1)
    mixed = jnp.einsum(
        "shqk,skhd->sqhd", expo.astype(jnp.bfloat16), v, preferred_element_type=jnp.float32
    )
    context = (mixed / jnp.transpose(totals, (0, 2, 1))[..., None]).astype(jnp.bfloat16)
    context = context.reshape(spec_mine, q_slots, heads_here * HD)
    context = jnp.swapaxes(context.reshape(spec_mine, n_z, -1), 0, 1)
    context_rows = lax.all_to_all(context, "z", 0, 0, tiled=True)
    context_rows = context_rows.reshape(n_band, spec_here, slots_here, heads_here * HD)
    context_rows = jnp.swapaxes(context_rows, 1, 2)
    out = jnp.einsum("bsjh,hd->bsjd", context_rows, w_out, preferred_element_type=jnp.bfloat16)
    attn_out = band_sum(out)
    state = (kept.astype(jnp.float32) + attn_out).astype(jnp.bfloat16)
    mlp_in = band_gather(normed(state, mlp_gain))
    gate = jnp.einsum("bsjd,df->bsjf", mlp_in, w_gate, preferred_element_type=jnp.float32)
    upper = jnp.einsum("bsjd,df->bsjf", mlp_in, w_up, preferred_element_type=jnp.float32)
    hidden = (jax.nn.silu(gate) * upper).astype(jnp.bfloat16)
    out = jnp.einsum("bsjf,fd->bsjd", hidden, w_down, preferred_element_type=jnp.bfloat16)
    mlp_out = band_sum(out)
    encoded = (state.astype(jnp.float32) + mlp_out).astype(jnp.bfloat16)
    chosen = (
        jnp.arange(pixels.shape[0], dtype=jnp.int32)[:, None] == clear_index[None, :]
    ) & live_here[None, :]
    placed = jnp.einsum(
        "pc,csd->psd", chosen.astype(jnp.bfloat16), encoded, preferred_element_type=jnp.float32
    ).astype(jnp.bfloat16)
    taken = jnp.any(chosen, axis=1)
    return jnp.where(taken[:, None, None], placed, pixels)


def solution(mesh):
    n_band, n_pix = mesh.devices.shape
    split = Mesh(mesh.devices.reshape(n_band, n_pix // 2, 2), ("band", "z", "c"))
    pix = ("z", "c")
    return jax.shard_map(
        shards,
        mesh=split,
        in_specs=(
            P(pix, "band", None),
            P(pix),
            P(pix),
            P(),
            P(None, "band"),
            P(None, "band"),
            P(None, "band"),
            P("band", None),
            P(),
            P(None, "band"),
            P(None, "band"),
            P("band", None),
        ),
        out_specs=P(pix, "band", None),
        check_vma=False,
    )
```

```python
import jax
import jax.numpy as jnp
from jax import lax
from jax.sharding import Mesh, PartitionSpec as P

HD = 64


def normed(rows, gain):
    full = rows.astype(jnp.float32)
    scaled = full * lax.rsqrt(jnp.mean(full * full, axis=-1, keepdims=True) + 1e-05)
    return (scaled * gain).astype(jnp.bfloat16)


def band_gather(rows):
    n = lax.axis_size("band")
    sent = jnp.broadcast_to(rows[None], (n,) + rows.shape)
    return lax.all_to_all(sent, "band", 0, 0, tiled=True)


def band_sum(part):
    got = lax.all_to_all(part, "band", 0, 0, tiled=True)
    return jnp.sum(got.astype(jnp.float32), axis=0)


def shards(
    pixels,
    clear_count,
    clear_index,
    attn_gain,
    w_query,
    w_key,
    w_value,
    w_out,
    mlp_gain,
    w_gate,
    w_up,
    w_down,
):
    own_count = clear_count[0]
    kept = jnp.take(pixels, clear_index, axis=0, mode="clip")
    slots_here, spec_here, width = kept.shape
    n_band = lax.axis_size("band")
    spec = n_band * spec_here
    attn_in = band_gather(jnp.take(normed(pixels, attn_gain), clear_index, axis=0, mode="clip"))
    flat = attn_in.reshape(-1, width)
    heads_here = w_query.shape[1] // HD

    live_here = jnp.arange(slots_here, dtype=jnp.int32) < own_count
    w_qkv = jnp.concatenate([w_query, w_key, w_value], axis=1)
    qkv = jnp.dot(flat, w_qkv, preferred_element_type=jnp.bfloat16)
    qkv = jnp.swapaxes(qkv.reshape(n_band, slots_here, spec_here, -1), 1, 2)
    width_qkv = qkv.shape[-1]
    n_flag = 64
    flags = jnp.pad(live_here.astype(jnp.bfloat16), (0, n_flag - slots_here))
    flags = jnp.broadcast_to(flags, (n_band, spec_here, n_flag))
    payload = jnp.concatenate([qkv.reshape(n_band, spec_here, -1), flags], axis=2)
    n_z = lax.axis_size("z")
    spec_mine = spec // n_z
    mine = lax.all_to_all(payload.reshape(n_z, spec_mine, -1), "z", 0, 0, tiled=True)
    live_mine = mine[:, 0, slots_here * width_qkv :]
    mine = mine[..., : slots_here * width_qkv].reshape(n_z, spec_mine, slots_here, width_qkv)
    mine = jnp.swapaxes(mine, 0, 1)
    kv = mine[..., heads_here * HD :]
    flag_rows = jnp.pad(live_mine, ((0, 0), (0, kv.shape[-1] - n_flag)))
    kv_flag = jnp.concatenate([kv, jnp.broadcast_to(flag_rows[None, :, None], (spec_mine,) + flag_rows.shape[:1] + (1, kv.shape[-1]))], axis=2)
    other = lax.ppermute(kv_flag, "c", [(0, 1), (1, 0)])
    q_slots = n_z * slots_here
    q = mine[:, :, :slots_here, : heads_here * HD].reshape(spec_mine, q_slots, heads_here, HD)

    def scores_of(part):
        k_part = part[:, :, :slots_here, : heads_here * HD].reshape(spec_mine, -1, heads_here, HD)
        return jnp.einsum("sqhd,skhd->shqk", q, k_part, preferred_element_type=jnp.float32)

    scores = jnp.concatenate([scores_of(kv_flag), scores_of(other)], axis=-1) * HD ** (-0.5)
    kv_flag = jnp.concatenate([kv_flag, other], axis=1)
    live = (kv_flag[0, :, slots_here, :slots_here] > 0.5).reshape(-1)
    kv = kv_flag[:, :, :slots_here].reshape(spec_mine, -1, 2 * heads_here * HD)
    v = kv[..., heads_here * HD :].reshape(spec_mine, -1, heads_here, HD)
    masked = jnp.where(live[None, None, None, :], scores, -1e30)
    top = jnp.max(masked, axis=-1)
    expo = jnp.where(live[None, None, None, :], jnp.exp(masked - top[..., None]), 0.0)
    totals = jnp.sum(expo, axis=-1)
    mixed = jnp.einsum(
        "shqk,skhd->sqhd", expo.astype(jnp.bfloat16), v, preferred_element_type=jnp.float32
    )
    context = (mixed / jnp.transpose(totals, (0, 2, 1))[..., None]).astype(jnp.bfloat16)
    context = context.reshape(spec_mine, q_slots, heads_here * HD)
    context = jnp.swapaxes(context.reshape(spec_mine, n_z, -1), 0, 1)
    context_rows = lax.all_to_all(context, "z", 0, 0, tiled=True)
    context_rows = context_rows.reshape(n_band, spec_here, slots_here, heads_here * HD)
    context_rows = jnp.swapaxes(context_rows, 1, 2)
    out = jnp.einsum("bsjh,hd->bsjd", context_rows, w_out, preferred_element_type=jnp.bfloat16)
    attn_out = band_sum(out)
    state = (kept.astype(jnp.float32) + attn_out).astype(jnp.bfloat16)
    mlp_in = band_gather(normed(state, mlp_gain))
    w_gate_up = jnp.concatenate([w_gate, w_up], axis=1)
    both = jnp.einsum("bsjd,df->bsjf", mlp_in, w_gate_up, preferred_element_type=jnp.float32)
    gate, upper = both[..., : w_gate.shape[1]], both[..., w_gate.shape[1] :]
    hidden = (jax.nn.silu(gate) * upper).astype(jnp.bfloat16)
    out = jnp.einsum("bsjf,fd->bsjd", hidden, w_down, preferred_element_type=jnp.bfloat16)
    mlp_out = band_sum(out)
    encoded = (state.astype(jnp.float32) + mlp_out).astype(jnp.bfloat16)
    chosen = (
        jnp.arange(pixels.shape[0], dtype=jnp.int32)[:, None] == clear_index[None, :]
    ) & live_here[None, :]
    placed = jnp.einsum(
        "pc,csd->psd", chosen.astype(jnp.bfloat16), encoded, preferred_element_type=jnp.float32
    ).astype(jnp.bfloat16)
    taken = jnp.any(chosen, axis=1)
    return jnp.where(taken[:, None, None], placed, pixels)


def solution(mesh):
    n_band, n_pix = mesh.devices.shape
    split = Mesh(mesh.devices.reshape(n_band, n_pix // 2, 2), ("band", "z", "c"))
    pix = ("z", "c")
    return jax.shard_map(
        shards,
        mesh=split,
        in_specs=(
            P(pix, "band", None),
            P(pix),
            P(pix),
            P(),
            P(None, "band"),
            P(None, "band"),
            P(None, "band"),
            P("band", None),
            P(),
            P(None, "band"),
            P(None, "band"),
            P("band", None),
        ),
        out_specs=P(pix, "band", None),
        check_vma=False,
    )
```

```python
import jax
import jax.numpy as jnp
from jax import lax
from jax.sharding import Mesh, PartitionSpec as P

HD = 64


def normed(rows, gain):
    full = rows.astype(jnp.float32)
    scaled = full * lax.rsqrt(jnp.mean(full * full, axis=-1, keepdims=True) + 1e-05)
    return (scaled * gain).astype(jnp.bfloat16)


def band_gather(rows):
    n = lax.axis_size("band")
    sent = jnp.broadcast_to(rows[None], (n,) + rows.shape)
    return lax.all_to_all(sent, "band", 0, 0, tiled=True)


def band_sum(part):
    got = lax.all_to_all(part, "band", 0, 0, tiled=True)
    return jnp.sum(got.astype(jnp.float32), axis=0)


def shards(
    pixels,
    clear_count,
    clear_index,
    attn_gain,
    w_query,
    w_key,
    w_value,
    w_out,
    mlp_gain,
    w_gate,
    w_up,
    w_down,
):
    own_count = clear_count[0]
    kept = jnp.take(pixels, clear_index, axis=0, mode="clip")
    slots_here, spec_here, width = kept.shape
    n_band = lax.axis_size("band")
    spec = n_band * spec_here
    attn_in = normed(band_gather(kept), attn_gain)
    flat = attn_in.reshape(-1, width)
    heads_here = w_query.shape[1] // HD

    live_here = jnp.arange(slots_here, dtype=jnp.int32) < own_count
    w_qkv = jnp.concatenate([w_query, w_key, w_value], axis=1)
    qkv = jnp.dot(flat, w_qkv, preferred_element_type=jnp.bfloat16)
    qkv = jnp.swapaxes(qkv.reshape(n_band, slots_here, spec_here, -1), 1, 2)
    width_qkv = qkv.shape[-1]
    n_flag = 64
    flags = jnp.pad(live_here.astype(jnp.bfloat16), (0, n_flag - slots_here))
    flags = jnp.broadcast_to(flags, (n_band, spec_here, n_flag))
    payload = jnp.concatenate([qkv.reshape(n_band, spec_here, -1), flags], axis=2)
    n_z = lax.axis_size("z")
    spec_mine = spec // n_z
    mine = lax.all_to_all(payload.reshape(n_z, spec_mine, -1), "z", 0, 0, tiled=True)
    live_mine = mine[:, 0, slots_here * width_qkv :]
    mine = mine[..., : slots_here * width_qkv].reshape(n_z, spec_mine, slots_here, width_qkv)
    mine = jnp.swapaxes(mine, 0, 1)
    kv = mine[..., heads_here * HD :]
    flag_rows = jnp.pad(live_mine, ((0, 0), (0, kv.shape[-1] - n_flag)))
    kv_flag = jnp.concatenate([kv, jnp.broadcast_to(flag_rows[None, :, None], (spec_mine,) + flag_rows.shape[:1] + (1, kv.shape[-1]))], axis=2)
    other = lax.ppermute(kv_flag, "c", [(0, 1), (1, 0)])
    q_slots = n_z * slots_here
    q = mine[:, :, :slots_here, : heads_here * HD].reshape(spec_mine, q_slots, heads_here, HD)

    def scores_of(part):
        k_part = part[:, :, :slots_here, : heads_here * HD].reshape(spec_mine, -1, heads_here, HD)
        return jnp.einsum("sqhd,skhd->shqk", q, k_part, preferred_element_type=jnp.float32)

    scores = jnp.concatenate([scores_of(kv_flag), scores_of(other)], axis=-1) * HD ** (-0.5)
    kv_flag = jnp.concatenate([kv_flag, other], axis=1)
    live = (kv_flag[0, :, slots_here, :slots_here] > 0.5).reshape(-1)
    kv = kv_flag[:, :, :slots_here].reshape(spec_mine, -1, 2 * heads_here * HD)
    v = kv[..., heads_here * HD :].reshape(spec_mine, -1, heads_here, HD)
    masked = jnp.where(live[None, None, None, :], scores, -1e30)
    top = jnp.max(masked, axis=-1)
    expo = jnp.where(live[None, None, None, :], jnp.exp(masked - top[..., None]), 0.0)
    totals = jnp.sum(expo, axis=-1)
    mixed = jnp.einsum(
        "shqk,skhd->sqhd", expo.astype(jnp.bfloat16), v, preferred_element_type=jnp.float32
    )
    context = (mixed / jnp.transpose(totals, (0, 2, 1))[..., None]).astype(jnp.bfloat16)
    context = context.reshape(spec_mine, q_slots, heads_here * HD)
    context = jnp.swapaxes(context.reshape(spec_mine, n_z, -1), 0, 1)
    context_rows = lax.all_to_all(context, "z", 0, 0, tiled=True)
    context_rows = context_rows.reshape(n_band, spec_here, slots_here, heads_here * HD)
    context_rows = jnp.swapaxes(context_rows, 1, 2)
    out = jnp.einsum("bsjh,hd->bsjd", context_rows, w_out, preferred_element_type=jnp.bfloat16)
    attn_out = band_sum(out)
    state = (kept.astype(jnp.float32) + attn_out).astype(jnp.bfloat16)
    mlp_in = band_gather(normed(state, mlp_gain))
    w_gate_up = jnp.concatenate([w_gate, w_up], axis=1)
    both = jnp.einsum("bsjd,df->bsjf", mlp_in, w_gate_up, preferred_element_type=jnp.float32)
    gate, upper = both[..., : w_gate.shape[1]], both[..., w_gate.shape[1] :]
    hidden = (jax.nn.silu(gate) * upper).astype(jnp.bfloat16)
    out = jnp.einsum("bsjf,fd->bsjd", hidden, w_down, preferred_element_type=jnp.bfloat16)
    mlp_out = band_sum(out)
    encoded = (state.astype(jnp.float32) + mlp_out).astype(jnp.bfloat16)
    chosen = (
        jnp.arange(pixels.shape[0], dtype=jnp.int32)[:, None] == clear_index[None, :]
    ) & live_here[None, :]
    placed = jnp.einsum(
        "pc,csd->psd", chosen.astype(jnp.bfloat16), encoded, preferred_element_type=jnp.float32
    ).astype(jnp.bfloat16)
    taken = jnp.any(chosen, axis=1)
    return jnp.where(taken[:, None, None], placed, pixels)


def solution(mesh):
    n_band, n_pix = mesh.devices.shape
    split = Mesh(mesh.devices.reshape(n_band, n_pix // 2, 2), ("band", "z", "c"))
    pix = ("z", "c")
    return jax.shard_map(
        shards,
        mesh=split,
        in_specs=(
            P(pix, "band", None),
            P(pix),
            P(pix),
            P(),
            P(None, "band"),
            P(None, "band"),
            P(None, "band"),
            P("band", None),
            P(),
            P(None, "band"),
            P(None, "band"),
            P("band", None),
        ),
        out_specs=P(pix, "band", None),
        check_vma=False,
    )
```

```python
import jax
import jax.numpy as jnp
from jax import lax
from jax.sharding import Mesh, PartitionSpec as P

HD = 64


def normed(rows, gain):
    full = rows.astype(jnp.float32)
    scaled = full * lax.rsqrt(jnp.mean(full * full, axis=-1, keepdims=True) + 1e-05)
    return (scaled * gain).astype(jnp.bfloat16)


def band_gather(rows):
    n = lax.axis_size("band")
    sent = jnp.broadcast_to(rows[None], (n,) + rows.shape)
    return lax.all_to_all(sent, "band", 0, 0, tiled=True)


def band_sum(part):
    got = lax.all_to_all(part, "band", 0, 0, tiled=True)
    return jnp.sum(got.astype(jnp.float32), axis=0)


def shards(
    pixels,
    clear_count,
    clear_index,
    attn_gain,
    w_query,
    w_key,
    w_value,
    w_out,
    mlp_gain,
    w_gate,
    w_up,
    w_down,
):
    own_count = clear_count[0]
    kept = jnp.take(pixels, clear_index, axis=0, mode="clip")
    slots_here, spec_here, width = kept.shape
    n_band = lax.axis_size("band")
    spec = n_band * spec_here
    attn_in = normed(band_gather(kept), attn_gain)
    flat = attn_in.reshape(-1, width)
    heads_here = w_query.shape[1] // HD

    live_here = jnp.arange(slots_here, dtype=jnp.int32) < own_count
    w_qkv = jnp.concatenate([w_query, w_key, w_value], axis=1)
    qkv = jnp.dot(flat, w_qkv, preferred_element_type=jnp.bfloat16)
    qkv = jnp.swapaxes(qkv.reshape(n_band, slots_here, spec_here, -1), 1, 2)
    width_qkv = qkv.shape[-1]
    n_flag = 64
    flags = jnp.pad(live_here.astype(jnp.bfloat16), (0, n_flag - slots_here))
    flags = jnp.broadcast_to(flags, (n_band, spec_here, n_flag))
    payload = jnp.concatenate([qkv.reshape(n_band, spec_here, -1), flags], axis=2)
    n_z = lax.axis_size("z")
    spec_mine = spec // n_z
    mine = lax.all_to_all(payload.reshape(n_z, spec_mine, -1), "z", 0, 0, tiled=True)
    live_mine = mine[:, 0, slots_here * width_qkv :]
    mine = mine[..., : slots_here * width_qkv].reshape(n_z, spec_mine, slots_here, width_qkv)
    mine = jnp.swapaxes(mine, 0, 1)
    kv = mine[..., heads_here * HD :]
    flag_rows = jnp.pad(live_mine, ((0, 0), (0, kv.shape[-1] - n_flag)))
    kv_flag = jnp.concatenate([kv, jnp.broadcast_to(flag_rows[None, :, None], (spec_mine,) + flag_rows.shape[:1] + (1, kv.shape[-1]))], axis=2)
    other = lax.ppermute(kv_flag, "c", [(0, 1), (1, 0)])
    q_slots = n_z * slots_here
    q = mine[:, :, :slots_here, : heads_here * HD].reshape(spec_mine, q_slots, heads_here, HD)

    def scores_of(part):
        k_part = part[:, :, :slots_here, : heads_here * HD].reshape(spec_mine, -1, heads_here, HD)
        return jnp.einsum("sqhd,skhd->shqk", q, k_part, preferred_element_type=jnp.float32)

    scores = jnp.concatenate([scores_of(kv_flag), scores_of(other)], axis=-1) * HD ** (-0.5)
    kv_flag = jnp.concatenate([kv_flag, other], axis=1)
    live = (kv_flag[0, :, slots_here, :slots_here] > 0.5).reshape(-1)
    kv = kv_flag[:, :, :slots_here].reshape(spec_mine, -1, 2 * heads_here * HD)
    v = kv[..., heads_here * HD :].reshape(spec_mine, -1, heads_here, HD)
    masked = jnp.where(live[None, None, None, :], scores, -1e30)
    top = jnp.max(masked, axis=-1)
    expo = jnp.where(live[None, None, None, :], jnp.exp(masked - top[..., None]), 0.0)
    totals = jnp.sum(expo, axis=-1)
    mixed = jnp.einsum(
        "shqk,skhd->sqhd", expo.astype(jnp.bfloat16), v, preferred_element_type=jnp.float32
    )
    context = (mixed / jnp.transpose(totals, (0, 2, 1))[..., None]).astype(jnp.bfloat16)
    context = context.reshape(spec_mine, q_slots, heads_here * HD)
    context = jnp.swapaxes(context.reshape(spec_mine, n_z, -1), 0, 1)
    context_rows = lax.all_to_all(context, "z", 0, 0, tiled=True)
    context_rows = context_rows.reshape(n_band, spec_here, slots_here, heads_here * HD)
    context_rows = jnp.swapaxes(context_rows, 1, 2)
    out = jnp.einsum("bsjh,hd->bsjd", context_rows, w_out, preferred_element_type=jnp.bfloat16)
    attn_out = band_sum(out)
    state = (kept.astype(jnp.float32) + attn_out).astype(jnp.bfloat16)
    mlp_in = normed(band_gather(state), mlp_gain)
    w_gate_up = jnp.concatenate([w_gate, w_up], axis=1)
    both = jnp.einsum("bsjd,df->bsjf", mlp_in, w_gate_up, preferred_element_type=jnp.float32)
    gate, upper = both[..., : w_gate.shape[1]], both[..., w_gate.shape[1] :]
    hidden = (jax.nn.silu(gate) * upper).astype(jnp.bfloat16)
    out = jnp.einsum("bsjf,fd->bsjd", hidden, w_down, preferred_element_type=jnp.bfloat16)
    mlp_out = band_sum(out)
    encoded = (state.astype(jnp.float32) + mlp_out).astype(jnp.bfloat16)
    chosen = (
        jnp.arange(pixels.shape[0], dtype=jnp.int32)[:, None] == clear_index[None, :]
    ) & live_here[None, :]
    placed = jnp.einsum(
        "pc,csd->psd", chosen.astype(jnp.bfloat16), encoded, preferred_element_type=jnp.float32
    ).astype(jnp.bfloat16)
    taken = jnp.any(chosen, axis=1)
    return jnp.where(taken[:, None, None], placed, pixels)


def solution(mesh):
    n_band, n_pix = mesh.devices.shape
    split = Mesh(mesh.devices.reshape(n_band, n_pix // 2, 2), ("band", "z", "c"))
    pix = ("z", "c")
    return jax.shard_map(
        shards,
        mesh=split,
        in_specs=(
            P(pix, "band", None),
            P(pix),
            P(pix),
            P(),
            P(None, "band"),
            P(None, "band"),
            P(None, "band"),
            P("band", None),
            P(),
            P(None, "band"),
            P(None, "band"),
            P("band", None),
        ),
        out_specs=P(pix, "band", None),
        check_vma=False,
    )
```

```python
import jax
import jax.numpy as jnp
from jax import lax
from jax.sharding import Mesh, PartitionSpec as P

HD = 64


def normed(rows, gain):
    full = rows.astype(jnp.float32)
    scaled = full * lax.rsqrt(jnp.mean(full * full, axis=-1, keepdims=True) + 1e-05)
    return (scaled * gain).astype(jnp.bfloat16)


def band_gather(rows):
    n = lax.axis_size("band")
    sent = jnp.broadcast_to(rows[None], (n,) + rows.shape)
    return lax.all_to_all(sent, "band", 0, 0, tiled=True)


def band_sum(part):
    got = lax.all_to_all(part, "band", 0, 0, tiled=True)
    return jnp.sum(got.astype(jnp.float32), axis=0)


def shards(
    pixels,
    clear_count,
    clear_index,
    attn_gain,
    w_query,
    w_key,
    w_value,
    w_out,
    mlp_gain,
    w_gate,
    w_up,
    w_down,
):
    own_count = clear_count[0]
    kept = jnp.take(pixels, clear_index, axis=0, mode="clip")
    slots_here, spec_here, width = kept.shape
    n_band = lax.axis_size("band")
    spec = n_band * spec_here
    attn_in = normed(band_gather(kept), attn_gain)
    flat = attn_in.reshape(-1, width)
    heads_here = w_query.shape[1] // HD

    live_here = jnp.arange(slots_here, dtype=jnp.int32) < own_count
    w_qkv = jnp.concatenate([w_query, w_key, w_value], axis=1)
    qkv = jnp.dot(flat, w_qkv, preferred_element_type=jnp.bfloat16)
    qkv = jnp.swapaxes(qkv.reshape(n_band, slots_here, spec_here, -1), 1, 2)
    width_qkv = qkv.shape[-1]
    n_flag = 64
    flags = jnp.pad(live_here.astype(jnp.bfloat16), (0, n_flag - slots_here))
    flags = jnp.broadcast_to(flags, (n_band, spec_here, n_flag))
    payload = jnp.concatenate([qkv.reshape(n_band, spec_here, -1), flags], axis=2)
    n_z = lax.axis_size("z")
    spec_mine = spec // n_z
    mine = lax.all_to_all(payload.reshape(n_z, spec_mine, -1), "z", 0, 0, tiled=True)
    live_mine = mine[:, 0, slots_here * width_qkv :]
    mine = mine[..., : slots_here * width_qkv].reshape(n_z, spec_mine, slots_here, width_qkv)
    mine = jnp.swapaxes(mine, 0, 1)
    kv = mine[..., heads_here * HD :]
    flag_rows = jnp.pad(live_mine, ((0, 0), (0, kv.shape[-1] - n_flag)))
    kv_flag = jnp.concatenate([kv, jnp.broadcast_to(flag_rows[None, :, None], (spec_mine,) + flag_rows.shape[:1] + (1, kv.shape[-1]))], axis=2)
    other = lax.ppermute(kv_flag, "c", [(0, 1), (1, 0)])
    q_slots = n_z * slots_here
    q = mine[:, :, :slots_here, : heads_here * HD].reshape(spec_mine, q_slots, heads_here, HD)

    def scores_of(part):
        k_part = part[:, :, :slots_here, : heads_here * HD].reshape(spec_mine, -1, heads_here, HD)
        return jnp.einsum("sqhd,skhd->shqk", q, k_part, preferred_element_type=jnp.float32)

    scores = jnp.concatenate([scores_of(kv_flag), scores_of(other)], axis=-1) * HD ** (-0.5)
    kv_flag = jnp.concatenate([kv_flag, other], axis=1)
    live = (kv_flag[0, :, slots_here, :slots_here] > 0.5).reshape(-1)
    kv = kv_flag[:, :, :slots_here].reshape(spec_mine, -1, 2 * heads_here * HD)
    v = kv[..., heads_here * HD :].reshape(spec_mine, -1, heads_here, HD)
    masked = jnp.where(live[None, None, None, :], scores, -1e30)
    top = jnp.max(masked, axis=-1)
    expo = jnp.where(live[None, None, None, :], jnp.exp(masked - top[..., None]), 0.0)
    totals = jnp.sum(expo, axis=-1)
    mixed = jnp.einsum(
        "shqk,skhd->sqhd", expo.astype(jnp.bfloat16), v, preferred_element_type=jnp.float32
    )
    context = (mixed / jnp.transpose(totals, (0, 2, 1))[..., None]).astype(jnp.bfloat16)
    context = context.reshape(spec_mine, q_slots, heads_here * HD)
    context = jnp.swapaxes(context.reshape(spec_mine, n_z, -1), 0, 1)
    context_rows = lax.all_to_all(context, "z", 0, 0, tiled=True)
    context_rows = context_rows.reshape(n_band, spec_here, slots_here, heads_here * HD)
    context_rows = jnp.swapaxes(context_rows, 1, 2)
    out = jnp.einsum("bsjh,hd->bsjd", context_rows, w_out, preferred_element_type=jnp.bfloat16)
    attn_out = band_sum(out)
    state = (kept.astype(jnp.float32) + attn_out).astype(jnp.bfloat16)
    mlp_in = band_gather(normed(state, mlp_gain))
    w_gate_up = jnp.concatenate([w_gate, w_up], axis=1)
    both = jnp.einsum("bsjd,df->bsjf", mlp_in, w_gate_up, preferred_element_type=jnp.float32)
    gate, upper = both[..., : w_gate.shape[1]], both[..., w_gate.shape[1] :]
    hidden = (jax.nn.silu(gate) * upper).astype(jnp.bfloat16)
    out = jnp.einsum("bsjf,fd->bsjd", hidden, w_down, preferred_element_type=jnp.bfloat16)
    mlp_out = band_sum(out)
    encoded = (state.astype(jnp.float32) + mlp_out).astype(jnp.bfloat16)
    chosen = (
        jnp.arange(pixels.shape[0], dtype=jnp.int32)[:, None] == clear_index[None, :]
    ) & live_here[None, :]
    source = jnp.argmax(chosen, axis=1).astype(jnp.int32)
    taken = jnp.any(chosen, axis=1)
    placed = jnp.take(encoded, source, axis=0, mode="clip")
    return jnp.where(taken[:, None, None], placed, pixels)


def solution(mesh):
    n_band, n_pix = mesh.devices.shape
    split = Mesh(mesh.devices.reshape(n_band, n_pix // 2, 2), ("band", "z", "c"))
    pix = ("z", "c")
    return jax.shard_map(
        shards,
        mesh=split,
        in_specs=(
            P(pix, "band", None),
            P(pix),
            P(pix),
            P(),
            P(None, "band"),
            P(None, "band"),
            P(None, "band"),
            P("band", None),
            P(),
            P(None, "band"),
            P(None, "band"),
            P("band", None),
        ),
        out_specs=P(pix, "band", None),
        check_vma=False,
    )
```

```python
import jax
import jax.numpy as jnp
from jax import lax
from jax.sharding import Mesh, PartitionSpec as P

HD = 64


def normed(rows, gain):
    full = rows.astype(jnp.float32)
    scaled = full * lax.rsqrt(jnp.mean(full * full, axis=-1, keepdims=True) + 1e-05)
    return (scaled * gain).astype(jnp.bfloat16)


def band_gather(rows):
    n = lax.axis_size("band")
    sent = jnp.broadcast_to(rows[None], (n,) + rows.shape)
    return lax.all_to_all(sent, "band", 0, 0, tiled=True)


def band_sum(part):
    got = lax.all_to_all(part, "band", 0, 0, tiled=True)
    return jnp.sum(got.astype(jnp.float32), axis=0)


def shards(
    pixels,
    clear_count,
    clear_index,
    attn_gain,
    w_query,
    w_key,
    w_value,
    w_out,
    mlp_gain,
    w_gate,
    w_up,
    w_down,
):
    own_count = clear_count[0]
    kept = jnp.take(pixels, clear_index, axis=0, mode="clip")
    slots_here, spec_here, width = kept.shape
    n_band = lax.axis_size("band")
    spec = n_band * spec_here
    sent = jnp.take(pixels, jnp.tile(clear_index, n_band), axis=0, mode="clip")
    sent = sent.reshape((n_band,) + kept.shape)
    attn_in = normed(lax.all_to_all(sent, "band", 0, 0, tiled=True), attn_gain)
    flat = attn_in.reshape(-1, width)
    heads_here = w_query.shape[1] // HD

    live_here = jnp.arange(slots_here, dtype=jnp.int32) < own_count
    w_qkv = jnp.concatenate([w_query, w_key, w_value], axis=1)
    qkv = jnp.dot(flat, w_qkv, preferred_element_type=jnp.bfloat16)
    qkv = jnp.swapaxes(qkv.reshape(n_band, slots_here, spec_here, -1), 1, 2)
    width_qkv = qkv.shape[-1]
    n_flag = 64
    flags = jnp.pad(live_here.astype(jnp.bfloat16), (0, n_flag - slots_here))
    flags = jnp.broadcast_to(flags, (n_band, spec_here, n_flag))
    payload = jnp.concatenate([qkv.reshape(n_band, spec_here, -1), flags], axis=2)
    n_z = lax.axis_size("z")
    spec_mine = spec // n_z
    mine = lax.all_to_all(payload.reshape(n_z, spec_mine, -1), "z", 0, 0, tiled=True)
    live_mine = mine[:, 0, slots_here * width_qkv :]
    mine = mine[..., : slots_here * width_qkv].reshape(n_z, spec_mine, slots_here, width_qkv)
    mine = jnp.swapaxes(mine, 0, 1)
    kv = mine[..., heads_here * HD :]
    flag_rows = jnp.pad(live_mine, ((0, 0), (0, kv.shape[-1] - n_flag)))
    kv_flag = jnp.concatenate([kv, jnp.broadcast_to(flag_rows[None, :, None], (spec_mine,) + flag_rows.shape[:1] + (1, kv.shape[-1]))], axis=2)
    other = lax.ppermute(kv_flag, "c", [(0, 1), (1, 0)])
    q_slots = n_z * slots_here
    q = mine[:, :, :slots_here, : heads_here * HD].reshape(spec_mine, q_slots, heads_here, HD)

    def scores_of(part):
        k_part = part[:, :, :slots_here, : heads_here * HD].reshape(spec_mine, -1, heads_here, HD)
        return jnp.einsum("sqhd,skhd->shqk", q, k_part, preferred_element_type=jnp.float32)

    scores = jnp.concatenate([scores_of(kv_flag), scores_of(other)], axis=-1) * HD ** (-0.5)
    kv_flag = jnp.concatenate([kv_flag, other], axis=1)
    live = (kv_flag[0, :, slots_here, :slots_here] > 0.5).reshape(-1)
    kv = kv_flag[:, :, :slots_here].reshape(spec_mine, -1, 2 * heads_here * HD)
    v = kv[..., heads_here * HD :].reshape(spec_mine, -1, heads_here, HD)
    masked = jnp.where(live[None, None, None, :], scores, -1e30)
    top = jnp.max(masked, axis=-1)
    expo = jnp.where(live[None, None, None, :], jnp.exp(masked - top[..., None]), 0.0)
    totals = jnp.sum(expo, axis=-1)
    mixed = jnp.einsum(
        "shqk,skhd->sqhd", expo.astype(jnp.bfloat16), v, preferred_element_type=jnp.float32
    )
    context = (mixed / jnp.transpose(totals, (0, 2, 1))[..., None]).astype(jnp.bfloat16)
    context = context.reshape(spec_mine, q_slots, heads_here * HD)
    context = jnp.swapaxes(context.reshape(spec_mine, n_z, -1), 0, 1)
    context_rows = lax.all_to_all(context, "z", 0, 0, tiled=True)
    context_rows = context_rows.reshape(n_band, spec_here, slots_here, heads_here * HD)
    context_rows = jnp.swapaxes(context_rows, 1, 2)
    out = jnp.einsum("bsjh,hd->bsjd", context_rows, w_out, preferred_element_type=jnp.bfloat16)
    attn_out = band_sum(out)
    state = (kept.astype(jnp.float32) + attn_out).astype(jnp.bfloat16)
    mlp_in = band_gather(normed(state, mlp_gain))
    w_gate_up = jnp.concatenate([w_gate, w_up], axis=1)
    both = jnp.einsum("bsjd,df->bsjf", mlp_in, w_gate_up, preferred_element_type=jnp.float32)
    gate, upper = both[..., : w_gate.shape[1]], both[..., w_gate.shape[1] :]
    hidden = (jax.nn.silu(gate) * upper).astype(jnp.bfloat16)
    out = jnp.einsum("bsjf,fd->bsjd", hidden, w_down, preferred_element_type=jnp.bfloat16)
    mlp_out = band_sum(out)
    encoded = (state.astype(jnp.float32) + mlp_out).astype(jnp.bfloat16)
    chosen = (
        jnp.arange(pixels.shape[0], dtype=jnp.int32)[:, None] == clear_index[None, :]
    ) & live_here[None, :]
    placed = jnp.einsum(
        "pc,csd->psd", chosen.astype(jnp.bfloat16), encoded, preferred_element_type=jnp.float32
    ).astype(jnp.bfloat16)
    taken = jnp.any(chosen, axis=1)
    return jnp.where(taken[:, None, None], placed, pixels)


def solution(mesh):
    n_band, n_pix = mesh.devices.shape
    split = Mesh(mesh.devices.reshape(n_band, n_pix // 2, 2), ("band", "z", "c"))
    pix = ("z", "c")
    return jax.shard_map(
        shards,
        mesh=split,
        in_specs=(
            P(pix, "band", None),
            P(pix),
            P(pix),
            P(),
            P(None, "band"),
            P(None, "band"),
            P(None, "band"),
            P("band", None),
            P(),
            P(None, "band"),
            P(None, "band"),
            P("band", None),
        ),
        out_specs=P(pix, "band", None),
        check_vma=False,
    )
```
